512 devices in a mesh: space: 32 (over x, y_hi, core), tm: 16 (over z, y_lo).
Axes of the slice: x: 4, y: 8 (y_hi: 4, y_lo: 2; y = y_hi * 2 + y_lo), z: 8, core: 2. Of those that a mesh axis runs over, the one named last changes fastest.
Arguments:
- field: float32 [256, 32768], P('tm', 'space'), may hold values from -6 to 6
- momentum: float32 [256, 32768], P('tm', 'space'), may hold values from -6 to 6
- solution: float32 [256, 32768], P('tm', 'space'), may hold values from -6 to 6
- tiles: float32 [256, 6, 128, 128], P('space'), may hold values from -1 to 2
- columns: int32 [256, 6], P('space'), may hold values from 0 to 255, as said below
- neighbours: int32 [3, 32768], P(None, 'space'), may hold values from 0 to 32767, as said below
Outputs:
- field_out: float32 [256, 32768], P('tm', 'space')
- momentum_out: float32 [256, 32768], P('tm', 'space')
- fermion_force: float32 [256, 32768], P('tm', 'space')
The draws below stay inside these ranges and needn't reach their ends.
Inputs may be any that keep to these rules, and one draw needn't show every extreme that they name: Row r lists 6 different tile columns, the first of them r itself; the others lie outside the run of 8 tile rows that holds r (runs r // 8), and the rows of one run name at most 2 columns of any other run, exactly 2 for some run. The neighbour relation is symmetric, each site has three different neighbours, and each neighbour lies in the site's own run of 128 labels or in the run just before or after it, cyclically over the flake.
All inputs are finite; a program needn't handle non-finite values.
Results may differ from the reference program's by a relative error of at most 0.00014.
Values sent between devices are 32-bit elements; how exact they have to be, the bound alone decides.
No kernel may reach another device: no remote copies, remote signals or barrier semaphores. Data moves between devices by JAX's collectives and lax.ppermute only.
A program may use at most 64 MiB of HBM per device.

```python
import math
import jax
import jax.numpy as jnp
from jax import lax

TILE = 128
KT = 6
TILES_DEV = 8
NTILES = 256
SITES = 32768
NT = 256
N_SPACE = 32


def draw_tiles(key, part):
    subkey = jax.random.fold_in(key, 11)
    tile_shape = (NTILES, KT, TILE, TILE)
    values = jnp.clip(jax.random.normal(subkey, tile_shape, jnp.float32), -6.0, 6.0)
    values = values * (1.0 / math.sqrt(TILE * KT))
    diagonal_mask = (jnp.arange(KT)[:, None, None] == 0) & (jnp.arange(TILE)[:, None] == jnp.arange(TILE)[None, :])[None, :, :]
    return values + diagonal_mask.astype(jnp.float32)[None, :, :, :]


def draw_columns(key, part):
    rot_key = jax.random.fold_in(key, 23)
    local_key = jax.random.fold_in(key, 29)
    row_ids = jnp.arange(NTILES, dtype=jnp.int32)
    run_ids = row_ids // TILES_DEV
    inner = row_ids % TILES_DEV
    rotation = jax.random.randint(rot_key, (N_SPACE,), 0, N_SPACE - 1).astype(jnp.int32)[run_ids]
    entry = inner[:, None] * (KT - 1) + jnp.arange(KT - 1, dtype=jnp.int32)[None, :]
    owner_run = (run_ids[:, None] + 1 + (entry + rotation[:, None]) % (N_SPACE - 1)) % N_SPACE
    local_ids = jax.random.randint(local_key, (NTILES, KT - 1), 0, TILES_DEV).astype(jnp.int32)
    others = owner_run * TILES_DEV + local_ids
    return jnp.concatenate([row_ids[:, None], others], axis=1).astype(jnp.int32)


def draw_neighbours(key, part):
    subkey = jax.random.fold_in(key, 37)
    scores = jax.random.randint(subkey, (NTILES, TILE), 0, 1 << 20) * TILE + jnp.arange(TILE, dtype=jnp.int32)[None, :]
    order_in_row = jnp.argsort(scores, axis=1).astype(jnp.int32)
    row_ids = jnp.arange(NTILES, dtype=jnp.int32)[:, None] + jnp.zeros((1, TILE), jnp.int32)
    col_ids = jnp.zeros((NTILES, 1), jnp.int32) + jnp.arange(TILE, dtype=jnp.int32)[None, :]
    labels = row_ids * TILE + order_in_row
    left_nb = labels[row_ids, (col_ids - 1) % TILE]
    right_nb = labels[row_ids, (col_ids + 1) % TILE]
    vertical_row = jnp.where((row_ids + col_ids) % 2 == 0, row_ids + 1, row_ids - 1) % NTILES
    vertical_nb = labels[vertical_row, col_ids]
    stacked = jnp.stack([left_nb.reshape(-1), right_nb.reshape(-1), vertical_nb.reshape(-1)], axis=0)
    result = jnp.zeros((3, SITES), jnp.int32).at[:, labels.reshape(-1)].set(stacked)
    return result.astype(jnp.int32)


def level_of(rng, shape, pieces, least, largest):
    level, own = 1.0, jax.random.fold_in(rng, 6)
    for axis_at, blocks in pieces:
        steps = jnp.exp(jax.random.uniform(jax.random.fold_in(own, axis_at), (blocks,), jnp.float32, least / len(pieces), largest / len(pieces)))
        level = level * jnp.repeat(steps, shape[axis_at] // blocks).reshape([-1 if axis == axis_at else 1 for axis in range(len(shape))])
    return level


def normal_values(key, shape, scale, bound, cuts=(), held_as=jnp.bfloat16):
    values = jax.random.normal(key, shape, jnp.float32) * scale
    if len(cuts) > 0:
        values = level_of(key, shape, cuts, -0.22, 0.18) * values
    return jnp.clip(values, min=-bound, max=bound).astype(held_as)


def setup_inputs(seed: int = 0) -> dict:
    keys = jax.random.split(jax.random.key(seed), 7)
    field = normal_values(keys[0], (NT, SITES), 1.0, 6.0, ((0, 16), (1, 32)), jnp.float32)
    momentum = normal_values(keys[1], (NT, SITES), 1.0, 6.0, ((0, 16), (1, 32)), jnp.float32)
    solution = normal_values(keys[2], (NT, SITES), 1.0, 6.0, ((0, 16), (1, 32)), jnp.float32)
    tiles = draw_tiles(jax.random.fold_in(keys[6], 71), 0)
    columns = draw_columns(jax.random.fold_in(keys[6], 71), 0)
    neighbours = draw_neighbours(jax.random.fold_in(keys[6], 71), 0)
    return dict(field=field, momentum=momentum, solution=solution, tiles=tiles, columns=columns, neighbours=neighbours)


step_size = 0.5
hop_kappa = 0.5
coupling = 0.25


def apply_tiles(values, tiles, columns):
    slices = values.shape[0]
    blocks = values.reshape(slices, NTILES, TILE)
    picked = blocks[:, columns]
    mixed = jnp.einsum("rkij,trkj->tri", tiles, picked, precision=lax.Precision.HIGHEST)
    return mixed.reshape(slices, SITES)


def reference(field, momentum, solution, tiles, columns, neighbours):
    moment = momentum - 0.5 * step_size * apply_tiles(field, tiles, columns)
    field_one = field + step_size * moment
    moment = moment - step_size * apply_tiles(field_one, tiles, columns)
    field_two = field_one + step_size * moment
    moment = moment - 0.5 * step_size * apply_tiles(field_two, tiles, columns)
    hopped = solution + hop_kappa * (solution[:, neighbours[0]] + solution[:, neighbours[1]] + solution[:, neighbours[2]])
    earlier = jnp.concatenate([-hopped[-1:], hopped[:-1]], axis=0)
    link_factor = jnp.exp(coupling * field_two)
    shifted = solution - link_factor * earlier
    force = 2.0 * coupling * shifted * link_factor * earlier
    return field_two, moment, force
```

```python
import jax
import jax.numpy as jnp
from jax import lax
from jax.sharding import PartitionSpec as P

TILE = 128


step_size = 0.5
hop_kappa = 0.5
coupling = 0.25


def with_halo(block, sides, width):
    for axis, dim in sides:
        count = lax.axis_size(axis)
        forward = [(i, i + 1) for i in range(count - 1)]
        forward.append((count - 1, 0))
        backward = [(target, source) for source, target in forward]
        low = lax.ppermute(
            lax.slice_in_dim(block, block.shape[dim] - width, None, axis=dim), axis, forward
        )
        high = lax.ppermute(lax.slice_in_dim(block, 0, width, axis=dim), axis, backward)
        block = jnp.concatenate([low, block, high], axis=dim)
    return block


def from_behind(value, axis, steps):
    count = lax.axis_size(axis)
    pairs = [(source, (source + steps) % count) for source in range(count)]
    return lax.ppermute(value, axis, pairs)


def body(field, momentum, solution, tiles, columns, neighbours):
    slices = field.shape[0]
    tile_rows = tiles.shape[0]
    kept = tiles.shape[1]
    site_count = field.shape[1]
    space_count = lax.axis_size("space")
    me = lax.axis_index("space")

    run_of = columns // tile_rows
    local_id = columns % tile_rows
    remote = run_of != me
    runs = jnp.arange(space_count, dtype=jnp.int32)
    hit = remote[:, :, None] & (run_of[:, :, None] == runs[None, None, :])
    lo = jnp.min(jnp.where(hit, local_id[:, :, None], tile_rows), axis=(0, 1))
    hi = jnp.max(jnp.where(hit, local_id[:, :, None], -1), axis=(0, 1))
    lo = jnp.clip(lo, 0, tile_rows - 1)
    hi = jnp.clip(hi, 0, tile_rows - 1)
    request = jnp.stack([lo, hi], axis=1)
    wanted = lax.all_to_all(request, "space", 0, 0, tiled=True)
    send_ids = wanted.reshape(-1)
    slot = jnp.where(local_id == lo[run_of], 0, 1)
    pick = jnp.where(remote, tile_rows + run_of * 2 + slot, local_id).reshape(-1)

    def coulomb(values):
        own = values.reshape(slices, tile_rows, TILE).transpose(1, 0, 2)
        sent = jnp.take(own, send_ids, axis=0)
        got = lax.all_to_all(sent, "space", 0, 0, tiled=True)
        pool = jnp.concatenate([own, got], axis=0)
        picked = jnp.take(pool, pick, axis=0).reshape(tile_rows, kept, slices, TILE)
        mixed = jnp.einsum("rkij,rktj->tri", tiles, picked, precision=lax.Precision.HIGHEST)
        return mixed.reshape(slices, site_count)

    moment = momentum - 0.5 * step_size * coulomb(field)
    field_one = field + step_size * moment
    moment = moment - step_size * coulomb(field_one)
    field_two = field_one + step_size * moment
    moment = moment - 0.5 * step_size * coulomb(field_two)

    total_sites = site_count * space_count
    first_site = me * site_count
    lookup = (neighbours - first_site + TILE) % total_sites
    parity_sign = jnp.where(lax.axis_index("tm") == 0, -1.0, 1.0).astype(jnp.float32)
    widened = with_halo(solution, (("space", 1),), TILE)
    blocks = site_count // TILE
    starts = (jnp.arange(blocks, dtype=jnp.int32) * TILE)[:, None, None]
    offsets = lookup.reshape(3, blocks, TILE).transpose(1, 0, 2) - starts
    window = jnp.arange(3 * TILE, dtype=jnp.int32)[None, None, :, None]
    adjacency = jnp.sum((offsets[:, :, None, :] == window).astype(jnp.float32), axis=1)
    parts = widened.reshape(slices, blocks + 2, TILE)
    windows = jnp.concatenate([parts[:, :-2], parts[:, 1:-1], parts[:, 2:]], axis=2)
    beside = jnp.einsum("tbj,bji->tbi", windows, adjacency, precision=lax.Precision.HIGHEST)
    hopped = solution + hop_kappa * beside.reshape(slices, site_count)
    arrived = from_behind(hopped[-1:], "tm", 1)
    earlier = jnp.concatenate([parity_sign * arrived, hopped[:-1]], axis=0)
    link_factor = jnp.exp(coupling * field_two)
    shifted = solution - link_factor * earlier
    force = 2.0 * coupling * shifted * link_factor * earlier
    return (field_two, moment, force)


def solution(mesh):
    in_specs = (
        P("tm", "space"),
        P("tm", "space"),
        P("tm", "space"),
        P("space", None, None, None),
        P("space", None),
        P(None, "space"),
    )
    out_specs = (P("tm", "space"), P("tm", "space"), P("tm", "space"))
    return jax.shard_map(body, mesh=mesh, in_specs=in_specs, out_specs=out_specs, check_vma=False)
```

```python
import jax
import jax.numpy as jnp
from jax import lax
from jax.sharding import PartitionSpec as P
from jax.experimental import pallas as pl
from jax.experimental.pallas import tpu as pltpu

TILE = 128


step_size = 0.5
hop_kappa = 0.5
coupling = 0.25


def with_halo(block, sides, width):
    for axis, dim in sides:
        count = lax.axis_size(axis)
        forward = [(i, i + 1) for i in range(count - 1)]
        forward.append((count - 1, 0))
        backward = [(target, source) for source, target in forward]
        low = lax.ppermute(
            lax.slice_in_dim(block, block.shape[dim] - width, None, axis=dim), axis, forward
        )
        high = lax.ppermute(lax.slice_in_dim(block, 0, width, axis=dim), axis, backward)
        block = jnp.concatenate([low, block, high], axis=dim)
    return block


def from_behind(value, axis, steps):
    count = lax.axis_size(axis)
    pairs = [(source, (source + steps) % count) for source in range(count)]
    return lax.ppermute(value, axis, pairs)


def dot_t(a, b):
    return lax.dot_general(
        a, b, (((1,), (1,)), ((), ())),
        precision=lax.Precision.HIGHEST, preferred_element_type=jnp.float32,
    )


def substep(field, moment, got, tiles, pick, send_ids, scale, advance, send):
    slices, site_count = field.shape
    rows, kept = tiles.shape[0], tiles.shape[1]
    slots = send_ids.shape[0]

    def kernel(pick_ref, sid_ref, f_ref, p_ref, got_ref, tiles_ref, *refs):
        outs = list(refs)
        p_out = outs.pop(0)
        f_out = outs.pop(0) if advance else None
        send_out = outs.pop(0) if send else None
        held = outs.pop(0) if send else None
        for r in range(rows):
            cols = slice(r * TILE, (r + 1) * TILE)
            acc = dot_t(f_ref[:, cols], tiles_ref[r, 0])
            for k in range(1, kept):
                acc = acc + dot_t(got_ref[pick_ref[r * kept + k]], tiles_ref[r, k])
            p_new = p_ref[:, cols] - scale * acc
            p_out[:, cols] = p_new
            if advance:
                f_new = f_ref[:, cols] + step_size * p_new
                f_out[:, cols] = f_new
                if send:
                    held[r] = f_new
        if send:
            def copy_one(s, carry):
                send_out[s] = held[sid_ref[s]]
                return carry
            lax.fori_loop(0, slots, copy_one, 0)

    vmem = pl.BlockSpec(memory_space=pltpu.VMEM)
    smem = pl.BlockSpec(memory_space=pltpu.SMEM)
    out_shape = [jax.ShapeDtypeStruct(field.shape, jnp.float32)]
    if advance:
        out_shape.append(jax.ShapeDtypeStruct(field.shape, jnp.float32))
    scratch = []
    if send:
        out_shape.append(jax.ShapeDtypeStruct((slots, slices, TILE), jnp.float32))
        scratch.append(pltpu.VMEM((rows, slices, TILE), jnp.float32))
    return pl.pallas_call(
        kernel,
        out_shape=tuple(out_shape),
        in_specs=[smem, smem, vmem, vmem, vmem, vmem],
        out_specs=tuple([vmem] * len(out_shape)),
        scratch_shapes=scratch,
    )(pick, send_ids, field, moment, got, tiles)


def gather_tiles(values, send_ids):
    slices, site_count = values.shape
    rows = site_count // TILE
    slots = send_ids.shape[0]

    def kernel(sid_ref, v_ref, send_out, held):
        for r in range(rows):
            held[r] = v_ref[:, r * TILE:(r + 1) * TILE]

        def copy_one(s, carry):
            send_out[s] = held[sid_ref[s]]
            return carry
        lax.fori_loop(0, slots, copy_one, 0)

    return pl.pallas_call(
        kernel,
        out_shape=jax.ShapeDtypeStruct((slots, slices, TILE), jnp.float32),
        in_specs=[pl.BlockSpec(memory_space=pltpu.SMEM), pl.BlockSpec(memory_space=pltpu.VMEM)],
        out_specs=pl.BlockSpec(memory_space=pltpu.VMEM),
        scratch_shapes=[pltpu.VMEM((rows, slices, TILE), jnp.float32)],
    )(send_ids, values)


def body(field, momentum, solution, tiles, columns, neighbours):
    slices = field.shape[0]
    tile_rows = tiles.shape[0]
    kept = tiles.shape[1]
    site_count = field.shape[1]
    space_count = lax.axis_size("space")
    me = lax.axis_index("space")

    run_of = columns // tile_rows
    local_id = columns % tile_rows
    remote = run_of != me
    runs = jnp.arange(space_count, dtype=jnp.int32)
    hit = remote[:, :, None] & (run_of[:, :, None] == runs[None, None, :])
    lo = jnp.min(jnp.where(hit, local_id[:, :, None], tile_rows), axis=(0, 1))
    hi = jnp.max(jnp.where(hit, local_id[:, :, None], -1), axis=(0, 1))
    lo = jnp.clip(lo, 0, tile_rows - 1)
    hi = jnp.clip(hi, 0, tile_rows - 1)
    request = jnp.stack([lo, hi], axis=1)
    wanted = lax.all_to_all(request, "space", 0, 0, tiled=True)
    send_ids = wanted.reshape(-1)
    slot = jnp.where(local_id == lo[run_of], 0, 1)

    pick = jnp.where(remote, run_of * 2 + slot, 0).reshape(-1)

    def exchange(sent):
        return lax.all_to_all(sent, "space", 0, 0, tiled=True)

    got = exchange(gather_tiles(field, send_ids))
    moment, field_one, sent = substep(field, momentum, got, tiles, pick, send_ids, 0.5 * step_size, True, True)
    got = exchange(sent)
    moment, field_two, sent = substep(field_one, moment, got, tiles, pick, send_ids, step_size, True, True)
    got = exchange(sent)
    (moment,) = substep(field_two, moment, got, tiles, pick, send_ids, 0.5 * step_size, False, False)

    total_sites = site_count * space_count
    first_site = me * site_count
    lookup = (neighbours - first_site + TILE) % total_sites
    parity_sign = jnp.where(lax.axis_index("tm") == 0, -1.0, 1.0).astype(jnp.float32)
    widened = with_halo(solution, (("space", 1),), TILE)
    blocks = site_count // TILE
    starts = (jnp.arange(blocks, dtype=jnp.int32) * TILE)[:, None, None]
    offsets = lookup.reshape(3, blocks, TILE).transpose(1, 0, 2) - starts
    window = jnp.arange(3 * TILE, dtype=jnp.int32)[None, None, :, None]
    adjacency = jnp.sum((offsets[:, :, None, :] == window).astype(jnp.float32), axis=1)
    parts = widened.reshape(slices, blocks + 2, TILE)
    windows = jnp.concatenate([parts[:, :-2], parts[:, 1:-1], parts[:, 2:]], axis=2)
    beside = jnp.einsum("tbj,bji->tbi", windows, adjacency, precision=lax.Precision.HIGHEST)
    hopped = solution + hop_kappa * beside.reshape(slices, site_count)
    arrived = from_behind(hopped[-1:], "tm", 1)
    earlier = jnp.concatenate([parity_sign * arrived, hopped[:-1]], axis=0)
    link_factor = jnp.exp(coupling * field_two)
    shifted = solution - link_factor * earlier
    force = 2.0 * coupling * shifted * link_factor * earlier
    return (field_two, moment, force)


def solution(mesh):
    in_specs = (
        P("tm", "space"),
        P("tm", "space"),
        P("tm", "space"),
        P("space", None, None, None),
        P("space", None),
        P(None, "space"),
    )
    out_specs = (P("tm", "space"), P("tm", "space"), P("tm", "space"))
    return jax.shard_map(body, mesh=mesh, in_specs=in_specs, out_specs=out_specs, check_vma=False)
```

```python
import jax
import jax.numpy as jnp
from jax import lax
from jax.sharding import PartitionSpec as P
from jax.experimental import pallas as pl
from jax.experimental.pallas import tpu as pltpu

TILE = 128


step_size = 0.5
hop_kappa = 0.5
coupling = 0.25


def with_halo(block, sides, width):
    for axis, dim in sides:
        count = lax.axis_size(axis)
        forward = [(i, i + 1) for i in range(count - 1)]
        forward.append((count - 1, 0))
        backward = [(target, source) for source, target in forward]
        low = lax.ppermute(
            lax.slice_in_dim(block, block.shape[dim] - width, None, axis=dim), axis, forward
        )
        high = lax.ppermute(lax.slice_in_dim(block, 0, width, axis=dim), axis, backward)
        block = jnp.concatenate([low, block, high], axis=dim)
    return block


def from_behind(value, axis, steps):
    count = lax.axis_size(axis)
    pairs = [(source, (source + steps) % count) for source in range(count)]
    return lax.ppermute(value, axis, pairs)


def substep(field, moment, got, tiles, pick, send_ids, scale, advance, send):
    slices, site_count = field.shape
    rows, kept = tiles.shape[0], tiles.shape[1] // TILE
    slots = send_ids.shape[0]

    def kernel(pick_ref, sid_ref, f_ref, p_ref, got_ref, tiles_ref, *refs):
        outs = list(refs)
        p_out = outs.pop(0)
        f_out = outs.pop(0) if advance else None
        send_out = outs.pop(0) if send else None
        held = outs.pop(0) if send else None
        for r in range(rows):
            cols = slice(r * TILE, (r + 1) * TILE)
            pieces = [f_ref[:, cols]] + [got_ref[pick_ref[r * kept + k]] for k in range(1, kept)]
            acc = jnp.dot(
                jnp.concatenate(pieces, axis=1), tiles_ref[r],
                precision=lax.Precision.HIGHEST, preferred_element_type=jnp.float32,
            )
            p_new = p_ref[:, cols] - scale * acc
            p_out[:, cols] = p_new
            if advance:
                f_new = f_ref[:, cols] + step_size * p_new
                f_out[:, cols] = f_new
                if send:
                    held[r] = f_new
        if send:
            def copy_one(s, carry):
                send_out[s] = held[sid_ref[s]]
                return carry
            lax.fori_loop(0, slots, copy_one, 0)

    vmem = pl.BlockSpec(memory_space=pltpu.VMEM)
    smem = pl.BlockSpec(memory_space=pltpu.SMEM)
    out_shape = [jax.ShapeDtypeStruct(field.shape, jnp.float32)]
    if advance:
        out_shape.append(jax.ShapeDtypeStruct(field.shape, jnp.float32))
    scratch = []
    if send:
        out_shape.append(jax.ShapeDtypeStruct((slots, slices, TILE), jnp.float32))
        scratch.append(pltpu.VMEM((rows, slices, TILE), jnp.float32))
    return pl.pallas_call(
        kernel,
        out_shape=tuple(out_shape),
        in_specs=[smem, smem, vmem, vmem, vmem, vmem],
        out_specs=tuple([vmem] * len(out_shape)),
        scratch_shapes=scratch,
    )(pick, send_ids, field, moment, got, tiles)


def gather_tiles(values, send_ids):
    slices, site_count = values.shape
    rows = site_count // TILE
    slots = send_ids.shape[0]

    def kernel(sid_ref, v_ref, send_out, held):
        for r in range(rows):
            held[r] = v_ref[:, r * TILE:(r + 1) * TILE]

        def copy_one(s, carry):
            send_out[s] = held[sid_ref[s]]
            return carry
        lax.fori_loop(0, slots, copy_one, 0)

    return pl.pallas_call(
        kernel,
        out_shape=jax.ShapeDtypeStruct((slots, slices, TILE), jnp.float32),
        in_specs=[pl.BlockSpec(memory_space=pltpu.SMEM), pl.BlockSpec(memory_space=pltpu.VMEM)],
        out_specs=pl.BlockSpec(memory_space=pltpu.VMEM),
        scratch_shapes=[pltpu.VMEM((rows, slices, TILE), jnp.float32)],
    )(send_ids, values)


def body(field, momentum, solution, tiles, columns, neighbours):
    slices = field.shape[0]
    tile_rows = tiles.shape[0]
    kept = tiles.shape[1]
    site_count = field.shape[1]
    space_count = lax.axis_size("space")
    me = lax.axis_index("space")

    run_of = columns // tile_rows
    local_id = columns % tile_rows
    remote = run_of != me
    runs = jnp.arange(space_count, dtype=jnp.int32)
    hit = remote[:, :, None] & (run_of[:, :, None] == runs[None, None, :])
    lo = jnp.min(jnp.where(hit, local_id[:, :, None], tile_rows), axis=(0, 1))
    hi = jnp.max(jnp.where(hit, local_id[:, :, None], -1), axis=(0, 1))
    lo = jnp.clip(lo, 0, tile_rows - 1)
    hi = jnp.clip(hi, 0, tile_rows - 1)
    request = jnp.stack([lo, hi], axis=1)
    wanted = lax.all_to_all(request, "space", 0, 0, tiled=True)
    send_ids = wanted.reshape(-1)
    slot = jnp.where(local_id == lo[run_of], 0, 1)

    pick = jnp.where(remote, run_of * 2 + slot, 0).reshape(-1)

    def exchange(sent):
        return lax.all_to_all(sent, "space", 0, 0, tiled=True)

    tiles = tiles.transpose(0, 1, 3, 2).reshape(tile_rows, kept * TILE, TILE)
    got = exchange(gather_tiles(field, send_ids))
    moment, field_one, sent = substep(field, momentum, got, tiles, pick, send_ids, 0.5 * step_size, True, True)
    got = exchange(sent)
    moment, field_two, sent = substep(field_one, moment, got, tiles, pick, send_ids, step_size, True, True)
    got = exchange(sent)
    (moment,) = substep(field_two, moment, got, tiles, pick, send_ids, 0.5 * step_size, False, False)

    total_sites = site_count * space_count
    first_site = me * site_count
    lookup = (neighbours - first_site + TILE) % total_sites
    parity_sign = jnp.where(lax.axis_index("tm") == 0, -1.0, 1.0).astype(jnp.float32)
    widened = with_halo(solution, (("space", 1),), TILE)
    blocks = site_count // TILE
    starts = (jnp.arange(blocks, dtype=jnp.int32) * TILE)[:, None, None]
    offsets = lookup.reshape(3, blocks, TILE).transpose(1, 0, 2) - starts
    window = jnp.arange(3 * TILE, dtype=jnp.int32)[None, None, :, None]
    adjacency = jnp.sum((offsets[:, :, None, :] == window).astype(jnp.float32), axis=1)
    parts = widened.reshape(slices, blocks + 2, TILE)
    windows = jnp.concatenate([parts[:, :-2], parts[:, 1:-1], parts[:, 2:]], axis=2)
    beside = jnp.einsum("tbj,bji->tbi", windows, adjacency, precision=lax.Precision.HIGHEST)
    hopped = solution + hop_kappa * beside.reshape(slices, site_count)
    arrived = from_behind(hopped[-1:], "tm", 1)
    earlier = jnp.concatenate([parity_sign * arrived, hopped[:-1]], axis=0)
    link_factor = jnp.exp(coupling * field_two)
    shifted = solution - link_factor * earlier
    force = 2.0 * coupling * shifted * link_factor * earlier
    return (field_two, moment, force)


def solution(mesh):
    in_specs = (
        P("tm", "space"),
        P("tm", "space"),
        P("tm", "space"),
        P("space", None, None, None),
        P("space", None),
        P(None, "space"),
    )
    out_specs = (P("tm", "space"), P("tm", "space"), P("tm", "space"))
    return jax.shard_map(body, mesh=mesh, in_specs=in_specs, out_specs=out_specs, check_vma=False)
```

```python
import jax
import jax.numpy as jnp
from jax import lax
from jax.sharding import PartitionSpec as P
from jax.experimental import pallas as pl
from jax.experimental.pallas import tpu as pltpu

TILE = 128


step_size = 0.5
hop_kappa = 0.5
coupling = 0.25


def with_halo(block, sides, width):
    for axis, dim in sides:
        count = lax.axis_size(axis)
        forward = [(i, i + 1) for i in range(count - 1)]
        forward.append((count - 1, 0))
        backward = [(target, source) for source, target in forward]
        low = lax.ppermute(
            lax.slice_in_dim(block, block.shape[dim] - width, None, axis=dim), axis, forward
        )
        high = lax.ppermute(lax.slice_in_dim(block, 0, width, axis=dim), axis, backward)
        block = jnp.concatenate([low, block, high], axis=dim)
    return block


def from_behind(value, axis, steps):
    count = lax.axis_size(axis)
    pairs = [(source, (source + steps) % count) for source in range(count)]
    return lax.ppermute(value, axis, pairs)


def split_dot(a, b):
    a_hi = a.astype(jnp.bfloat16)
    a_lo = (a - a_hi.astype(jnp.float32)).astype(jnp.bfloat16)
    b_hi = b.astype(jnp.bfloat16)
    b_lo = (b - b_hi.astype(jnp.float32)).astype(jnp.bfloat16)

    def part(x, y):
        return jnp.dot(x, y, preferred_element_type=jnp.float32)

    return part(a_hi, b_hi) + (part(a_hi, b_lo) + part(a_lo, b_hi))


def substep(field, moment, got, tiles, pick, send_ids, scale, advance, send):
    slices, site_count = field.shape
    rows, kept = tiles.shape[0], tiles.shape[1] // TILE
    slots = send_ids.shape[0] * send_ids.shape[1]

    def kernel(pick_ref, sid_ref, f_ref, p_ref, got_ref, tiles_ref, *refs):
        outs = list(refs)
        p_out = outs.pop(0)
        f_out = outs.pop(0) if advance else None
        send_out = outs.pop(0) if send else None
        held = outs.pop(0) if send else None
        for r in range(rows):
            cols = slice(r * TILE, (r + 1) * TILE)
            pieces = [f_ref[:, cols]] + [got_ref[pick_ref[r, k]] for k in range(1, kept)]
            acc = split_dot(jnp.concatenate(pieces, axis=1), tiles_ref[r])
            p_new = p_ref[:, cols] - scale * acc
            p_out[:, cols] = p_new
            if advance:
                f_new = f_ref[:, cols] + step_size * p_new
                f_out[:, cols] = f_new
                if send:
                    held[r] = f_new
        if send:
            def copy_one(s, carry):
                send_out[s] = held[sid_ref[s // 2, s % 2]]
                return carry
            lax.fori_loop(0, slots, copy_one, 0)

    vmem = pl.BlockSpec(memory_space=pltpu.VMEM)
    smem = pl.BlockSpec(memory_space=pltpu.SMEM)
    out_shape = [jax.ShapeDtypeStruct(field.shape, jnp.float32)]
    if advance:
        out_shape.append(jax.ShapeDtypeStruct(field.shape, jnp.float32))
    scratch = []
    if send:
        out_shape.append(jax.ShapeDtypeStruct((slots, slices, TILE), jnp.float32))
        scratch.append(pltpu.VMEM((rows, slices, TILE), jnp.float32))
    return pl.pallas_call(
        kernel,
        out_shape=tuple(out_shape),
        in_specs=[smem, smem, vmem, vmem, vmem, vmem],
        out_specs=tuple([vmem] * len(out_shape)),
        scratch_shapes=scratch,
    )(pick, send_ids, field, moment, got, tiles)


def gather_tiles(values, send_ids):
    slices, site_count = values.shape
    rows = site_count // TILE
    slots = send_ids.shape[0] * send_ids.shape[1]

    def kernel(sid_ref, v_ref, send_out, held):
        for r in range(rows):
            held[r] = v_ref[:, r * TILE:(r + 1) * TILE]

        def copy_one(s, carry):
            send_out[s] = held[sid_ref[s // 2, s % 2]]
            return carry
        lax.fori_loop(0, slots, copy_one, 0)

    return pl.pallas_call(
        kernel,
        out_shape=jax.ShapeDtypeStruct((slots, slices, TILE), jnp.float32),
        in_specs=[pl.BlockSpec(memory_space=pltpu.SMEM), pl.BlockSpec(memory_space=pltpu.VMEM)],
        out_specs=pl.BlockSpec(memory_space=pltpu.VMEM),
        scratch_shapes=[pltpu.VMEM((rows, slices, TILE), jnp.float32)],
    )(send_ids, values)


def body(field, momentum, solution, tiles, columns, neighbours):
    slices = field.shape[0]
    tile_rows = tiles.shape[0]
    kept = tiles.shape[1]
    site_count = field.shape[1]
    space_count = lax.axis_size("space")
    me = lax.axis_index("space")

    run_of = columns // tile_rows
    local_id = columns % tile_rows
    remote = run_of != me
    runs = jnp.arange(space_count, dtype=jnp.int32)
    hit = remote[:, :, None] & (run_of[:, :, None] == runs[None, None, :])
    lo = jnp.min(jnp.where(hit, local_id[:, :, None], tile_rows), axis=(0, 1))
    hi = jnp.max(jnp.where(hit, local_id[:, :, None], -1), axis=(0, 1))
    lo = jnp.clip(lo, 0, tile_rows - 1)
    hi = jnp.clip(hi, 0, tile_rows - 1)
    request = jnp.stack([lo, hi], axis=1)
    send_ids = lax.all_to_all(request, "space", 0, 0)
    slot = jnp.where(local_id == lo[run_of], 0, 1)

    pick = jnp.where(remote, run_of * 2 + slot, 0)

    def exchange(sent):
        return lax.all_to_all(sent, "space", 0, 0, tiled=True)

    tiles = tiles.transpose(0, 1, 3, 2).reshape(tile_rows, kept * TILE, TILE)
    got = exchange(gather_tiles(field, send_ids))
    moment, field_one, sent = substep(field, momentum, got, tiles, pick, send_ids, 0.5 * step_size, True, True)
    got = exchange(sent)
    moment, field_two, sent = substep(field_one, moment, got, tiles, pick, send_ids, step_size, True, True)
    got = exchange(sent)
    (moment,) = substep(field_two, moment, got, tiles, pick, send_ids, 0.5 * step_size, False, False)

    total_sites = site_count * space_count
    first_site = me * site_count
    lookup = (neighbours - first_site + TILE) % total_sites
    parity_sign = jnp.where(lax.axis_index("tm") == 0, -1.0, 1.0).astype(jnp.float32)
    widened = with_halo(solution, (("space", 1),), TILE)
    blocks = site_count // TILE
    starts = (jnp.arange(blocks, dtype=jnp.int32) * TILE)[:, None, None]
    offsets = lookup.reshape(3, blocks, TILE).transpose(1, 0, 2) - starts
    window = jnp.arange(3 * TILE, dtype=jnp.int32)[None, None, :, None]
    adjacency = jnp.sum((offsets[:, :, None, :] == window).astype(jnp.float32), axis=1)
    parts = widened.reshape(slices, blocks + 2, TILE)
    windows = jnp.concatenate([parts[:, :-2], parts[:, 1:-1], parts[:, 2:]], axis=2)
    beside = jnp.einsum("tbj,bji->tbi", windows, adjacency, precision=lax.Precision.HIGHEST)
    hopped = solution + hop_kappa * beside.reshape(slices, site_count)
    arrived = from_behind(hopped[-1:], "tm", 1)
    earlier = jnp.concatenate([parity_sign * arrived, hopped[:-1]], axis=0)
    link_factor = jnp.exp(coupling * field_two)
    shifted = solution - link_factor * earlier
    force = 2.0 * coupling * shifted * link_factor * earlier
    return (field_two, moment, force)


def solution(mesh):
    in_specs = (
        P("tm", "space"),
        P("tm", "space"),
        P("tm", "space"),
        P("space", None, None, None),
        P("space", None),
        P(None, "space"),
    )
    out_specs = (P("tm", "space"), P("tm", "space"), P("tm", "space"))
    return jax.shard_map(body, mesh=mesh, in_specs=in_specs, out_specs=out_specs, check_vma=False)
```

```python
import jax
import jax.numpy as jnp
from jax import lax
from jax.sharding import PartitionSpec as P
from jax.experimental import pallas as pl
from jax.experimental.pallas import tpu as pltpu

TILE = 128


step_size = 0.5
hop_kappa = 0.5
coupling = 0.25


def with_halo(block, sides, width):
    for axis, dim in sides:
        count = lax.axis_size(axis)
        forward = [(i, i + 1) for i in range(count - 1)]
        forward.append((count - 1, 0))
        backward = [(target, source) for source, target in forward]
        low = lax.ppermute(
            lax.slice_in_dim(block, block.shape[dim] - width, None, axis=dim), axis, forward
        )
        high = lax.ppermute(lax.slice_in_dim(block, 0, width, axis=dim), axis, backward)
        block = jnp.concatenate([low, block, high], axis=dim)
    return block


def from_behind(value, axis, steps):
    count = lax.axis_size(axis)
    pairs = [(source, (source + steps) % count) for source in range(count)]
    return lax.ppermute(value, axis, pairs)


def split_dot(a, b):
    a_hi = a.astype(jnp.bfloat16)
    a_lo = (a - a_hi.astype(jnp.float32)).astype(jnp.bfloat16)
    b_hi = b.astype(jnp.bfloat16)
    b_lo = (b - b_hi.astype(jnp.float32)).astype(jnp.bfloat16)

    def part(x, y):
        return jnp.dot(x, y, preferred_element_type=jnp.float32)

    return part(a_hi, b_hi) + (part(a_hi, b_lo) + part(a_lo, b_hi))


def substep(field, moment, got, tiles, pick, send_ids, scale, advance, send):
    slices, site_count = field.shape
    rows, kept = tiles.shape[0], tiles.shape[1] // TILE
    slots = send_ids.shape[0] * send_ids.shape[1]

    def kernel(pick_ref, sid_ref, f_ref, p_ref, got_ref, tiles_hbm, *refs):
        outs = list(refs)
        p_out = outs.pop(0)
        f_out = outs.pop(0) if advance else None
        send_out = outs.pop(0) if send else None
        held = outs.pop(0) if send else None
        row_buf, row_sem = outs

        def fetch(r):
            return pltpu.make_async_copy(tiles_hbm.at[r], row_buf.at[r % 2], row_sem.at[r % 2])

        pending = fetch(0)
        pending.start()
        for r in range(rows):
            current = pending
            if r + 1 < rows:
                pending = fetch(r + 1)
                pending.start()
            current.wait()
            cols = slice(r * TILE, (r + 1) * TILE)
            pieces = [f_ref[:, cols]] + [got_ref[pick_ref[r, k]] for k in range(1, kept)]
            acc = split_dot(jnp.concatenate(pieces, axis=1), row_buf[r % 2])
            p_new = p_ref[:, cols] - scale * acc
            p_out[:, cols] = p_new
            if advance:
                f_new = f_ref[:, cols] + step_size * p_new
                f_out[:, cols] = f_new
                if send:
                    held[r] = f_new
        if send:
            def copy_one(s, carry):
                send_out[s] = held[sid_ref[s // 2, s % 2]]
                return carry
            lax.fori_loop(0, slots, copy_one, 0)

    vmem = pl.BlockSpec(memory_space=pltpu.VMEM)
    smem = pl.BlockSpec(memory_space=pltpu.SMEM)
    out_shape = [jax.ShapeDtypeStruct(field.shape, jnp.float32)]
    if advance:
        out_shape.append(jax.ShapeDtypeStruct(field.shape, jnp.float32))
    scratch = []
    if send:
        out_shape.append(jax.ShapeDtypeStruct((slots, slices, TILE), jnp.float32))
        scratch.append(pltpu.VMEM((rows, slices, TILE), jnp.float32))
    scratch.append(pltpu.VMEM((2, kept * TILE, TILE), jnp.float32))
    scratch.append(pltpu.SemaphoreType.DMA((2,)))
    return pl.pallas_call(
        kernel,
        out_shape=tuple(out_shape),
        in_specs=[smem, smem, vmem, vmem, vmem, pl.BlockSpec(memory_space=pl.ANY)],
        out_specs=tuple([vmem] * len(out_shape)),
        scratch_shapes=scratch,
    )(pick, send_ids, field, moment, got, tiles)


def gather_tiles(values, send_ids):
    slices, site_count = values.shape
    rows = site_count // TILE
    slots = send_ids.shape[0] * send_ids.shape[1]

    def kernel(sid_ref, v_ref, send_out, held):
        for r in range(rows):
            held[r] = v_ref[:, r * TILE:(r + 1) * TILE]

        def copy_one(s, carry):
            send_out[s] = held[sid_ref[s // 2, s % 2]]
            return carry
        lax.fori_loop(0, slots, copy_one, 0)

    return pl.pallas_call(
        kernel,
        out_shape=jax.ShapeDtypeStruct((slots, slices, TILE), jnp.float32),
        in_specs=[pl.BlockSpec(memory_space=pltpu.SMEM), pl.BlockSpec(memory_space=pltpu.VMEM)],
        out_specs=pl.BlockSpec(memory_space=pltpu.VMEM),
        scratch_shapes=[pltpu.VMEM((rows, slices, TILE), jnp.float32)],
    )(send_ids, values)


def body(field, momentum, solution, tiles, columns, neighbours):
    slices = field.shape[0]
    tile_rows = tiles.shape[0]
    kept = tiles.shape[1]
    site_count = field.shape[1]
    space_count = lax.axis_size("space")
    me = lax.axis_index("space")

    run_of = columns // tile_rows
    local_id = columns % tile_rows
    remote = run_of != me
    runs = jnp.arange(space_count, dtype=jnp.int32)
    hit = remote[:, :, None] & (run_of[:, :, None] == runs[None, None, :])
    lo = jnp.min(jnp.where(hit, local_id[:, :, None], tile_rows), axis=(0, 1))
    hi = jnp.max(jnp.where(hit, local_id[:, :, None], -1), axis=(0, 1))
    lo = jnp.clip(lo, 0, tile_rows - 1)
    hi = jnp.clip(hi, 0, tile_rows - 1)
    request = jnp.stack([lo, hi], axis=1)
    send_ids = lax.all_to_all(request, "space", 0, 0)
    slot = jnp.where(local_id == lo[run_of], 0, 1)

    pick = jnp.where(remote, run_of * 2 + slot, 0)

    def exchange(sent):
        return lax.all_to_all(sent, "space", 0, 0, tiled=True)

    tiles = tiles.transpose(0, 1, 3, 2).reshape(tile_rows, kept * TILE, TILE)
    got = exchange(gather_tiles(field, send_ids))
    moment, field_one, sent = substep(field, momentum, got, tiles, pick, send_ids, 0.5 * step_size, True, True)
    got = exchange(sent)
    moment, field_two, sent = substep(field_one, moment, got, tiles, pick, send_ids, step_size, True, True)
    got = exchange(sent)
    (moment,) = substep(field_two, moment, got, tiles, pick, send_ids, 0.5 * step_size, False, False)

    total_sites = site_count * space_count
    first_site = me * site_count
    lookup = (neighbours - first_site + TILE) % total_sites
    parity_sign = jnp.where(lax.axis_index("tm") == 0, -1.0, 1.0).astype(jnp.float32)
    widened = with_halo(solution, (("space", 1),), TILE)
    blocks = site_count // TILE
    starts = (jnp.arange(blocks, dtype=jnp.int32) * TILE)[:, None, None]
    offsets = lookup.reshape(3, blocks, TILE).transpose(1, 0, 2) - starts
    window = jnp.arange(3 * TILE, dtype=jnp.int32)[None, None, :, None]
    adjacency = jnp.sum((offsets[:, :, None, :] == window).astype(jnp.float32), axis=1)
    parts = widened.reshape(slices, blocks + 2, TILE)
    windows = jnp.concatenate([parts[:, :-2], parts[:, 1:-1], parts[:, 2:]], axis=2)
    beside = jnp.einsum("tbj,bji->tbi", windows, adjacency, precision=lax.Precision.HIGHEST)
    hopped = solution + hop_kappa * beside.reshape(slices, site_count)
    arrived = from_behind(hopped[-1:], "tm", 1)
    earlier = jnp.concatenate([parity_sign * arrived, hopped[:-1]], axis=0)
    link_factor = jnp.exp(coupling * field_two)
    shifted = solution - link_factor * earlier
    force = 2.0 * coupling * shifted * link_factor * earlier
    return (field_two, moment, force)


def solution(mesh):
    in_specs = (
        P("tm", "space"),
        P("tm", "space"),
        P("tm", "space"),
        P("space", None, None, None),
        P("space", None),
        P(None, "space"),
    )
    out_specs = (P("tm", "space"), P("tm", "space"), P("tm", "space"))
    return jax.shard_map(body, mesh=mesh, in_specs=in_specs, out_specs=out_specs, check_vma=False)
```

```python
import jax
import jax.numpy as jnp
from jax import lax
from jax.sharding import PartitionSpec as P
from jax.experimental import pallas as pl
from jax.experimental.pallas import tpu as pltpu

TILE = 128


step_size = 0.5
hop_kappa = 0.5
coupling = 0.25


def with_halo(block, sides, width):
    for axis, dim in sides:
        count = lax.axis_size(axis)
        forward = [(i, i + 1) for i in range(count - 1)]
        forward.append((count - 1, 0))
        backward = [(target, source) for source, target in forward]
        low = lax.ppermute(
            lax.slice_in_dim(block, block.shape[dim] - width, None, axis=dim), axis, forward
        )
        high = lax.ppermute(lax.slice_in_dim(block, 0, width, axis=dim), axis, backward)
        block = jnp.concatenate([low, block, high], axis=dim)
    return block


def from_behind(value, axis, steps):
    count = lax.axis_size(axis)
    pairs = [(source, (source + steps) % count) for source in range(count)]
    return lax.ppermute(value, axis, pairs)


def split_dot(a, b):
    a_hi = a.astype(jnp.bfloat16)
    a_lo = (a - a_hi.astype(jnp.float32)).astype(jnp.bfloat16)
    b_hi = b.astype(jnp.bfloat16)
    b_lo = (b - b_hi.astype(jnp.float32)).astype(jnp.bfloat16)

    def part(x, y):
        return jnp.dot(x, y, preferred_element_type=jnp.float32)

    return part(a_hi, b_hi) + (part(a_hi, b_lo) + part(a_lo, b_hi))


def substep(field, moment, got, tiles, pick, send_ids, scale, advance, send):
    slices, site_count = field.shape
    rows, kept = tiles.shape[0], tiles.shape[1] // TILE
    slots = send_ids.shape[0] * send_ids.shape[1]

    def kernel(pick_ref, sid_ref, f_ref, p_ref, got_ref, tiles_ref, *refs):
        outs = list(refs)
        p_out = outs.pop(0)
        f_out = outs.pop(0) if advance else None
        send_out = outs.pop(0) if send else None
        held = outs.pop(0) if send else None
        for r in range(rows):
            cols = slice(r * TILE, (r + 1) * TILE)
            pieces = [f_ref[:, cols]] + [got_ref[pick_ref[r, k]] for k in range(1, kept)]
            acc = split_dot(jnp.concatenate(pieces, axis=1), tiles_ref[r])
            p_new = p_ref[:, cols] - scale * acc
            p_out[:, cols] = p_new
            if advance:
                f_new = f_ref[:, cols] + step_size * p_new
                f_out[:, cols] = f_new
                if send:
                    held[r] = f_new
        if send:
            def copy_one(s, carry):
                send_out[s] = held[sid_ref[s // 2, s % 2]]
                return carry
            lax.fori_loop(0, slots, copy_one, 0)

    vmem = pl.BlockSpec(memory_space=pltpu.VMEM)
    smem = pl.BlockSpec(memory_space=pltpu.SMEM)
    out_shape = [jax.ShapeDtypeStruct(field.shape, jnp.float32)]
    if advance:
        out_shape.append(jax.ShapeDtypeStruct(field.shape, jnp.float32))
    scratch = []
    if send:
        out_shape.append(jax.ShapeDtypeStruct((slots, slices, TILE), jnp.float32))
        scratch.append(pltpu.VMEM((rows, slices, TILE), jnp.float32))
    return pl.pallas_call(
        kernel,
        out_shape=tuple(out_shape),
        in_specs=[smem, smem, vmem, vmem, vmem, vmem],
        out_specs=tuple([vmem] * len(out_shape)),
        scratch_shapes=scratch,
    )(pick, send_ids, field, moment, got, tiles)


def body(field, momentum, solution, tiles, columns, neighbours):
    slices = field.shape[0]
    tile_rows = tiles.shape[0]
    kept = tiles.shape[1]
    site_count = field.shape[1]
    space_count = lax.axis_size("space")
    me = lax.axis_index("space")

    run_of = columns // tile_rows
    local_id = columns % tile_rows
    remote = run_of != me
    runs = jnp.arange(space_count, dtype=jnp.int32)
    hit = remote[:, :, None] & (run_of[:, :, None] == runs[None, None, :])
    lo = jnp.min(jnp.where(hit, local_id[:, :, None], tile_rows), axis=(0, 1))
    hi = jnp.max(jnp.where(hit, local_id[:, :, None], -1), axis=(0, 1))
    lo = jnp.clip(lo, 0, tile_rows - 1)
    hi = jnp.clip(hi, 0, tile_rows - 1)
    request = jnp.stack([lo, hi], axis=1)
    send_ids = lax.all_to_all(request, "space", 0, 0)
    slot = jnp.where(local_id == lo[run_of], 0, 1)

    pick = jnp.where(remote, run_of * 2 + slot, 0)

    def exchange(sent):
        return lax.all_to_all(sent, "space", 0, 0, tiled=True)

    tiles = tiles.transpose(0, 1, 3, 2).reshape(tile_rows, kept * TILE, TILE)
    own = field.reshape(slices, tile_rows, TILE)
    first = jnp.take(own, send_ids.reshape(-1), axis=1, mode="clip").transpose(1, 0, 2)
    got = exchange(first)
    moment, field_one, sent = substep(field, momentum, got, tiles, pick, send_ids, 0.5 * step_size, True, True)
    got = exchange(sent)
    moment, field_two, sent = substep(field_one, moment, got, tiles, pick, send_ids, step_size, True, True)
    got = exchange(sent)
    (moment,) = substep(field_two, moment, got, tiles, pick, send_ids, 0.5 * step_size, False, False)

    total_sites = site_count * space_count
    first_site = me * site_count
    lookup = (neighbours - first_site + TILE) % total_sites
    parity_sign = jnp.where(lax.axis_index("tm") == 0, -1.0, 1.0).astype(jnp.float32)
    widened = with_halo(solution, (("space", 1),), TILE)
    blocks = site_count // TILE
    starts = (jnp.arange(blocks, dtype=jnp.int32) * TILE)[:, None, None]
    offsets = lookup.reshape(3, blocks, TILE).transpose(1, 0, 2) - starts
    window = jnp.arange(3 * TILE, dtype=jnp.int32)[None, None, :, None]
    adjacency = jnp.sum((offsets[:, :, None, :] == window).astype(jnp.float32), axis=1)
    parts = widened.reshape(slices, blocks + 2, TILE)
    windows = jnp.concatenate([parts[:, :-2], parts[:, 1:-1], parts[:, 2:]], axis=2)
    beside = jnp.einsum("tbj,bji->tbi", windows, adjacency, precision=lax.Precision.HIGHEST)
    hopped = solution + hop_kappa * beside.reshape(slices, site_count)
    arrived = from_behind(hopped[-1:], "tm", 1)
    earlier = jnp.concatenate([parity_sign * arrived, hopped[:-1]], axis=0)
    link_factor = jnp.exp(coupling * field_two)
    shifted = solution - link_factor * earlier
    force = 2.0 * coupling * shifted * link_factor * earlier
    return (field_two, moment, force)


def solution(mesh):
    in_specs = (
        P("tm", "space"),
        P("tm", "space"),
        P("tm", "space"),
        P("space", None, None, None),
        P("space", None),
        P(None, "space"),
    )
    out_specs = (P("tm", "space"), P("tm", "space"), P("tm", "space"))
    return jax.shard_map(body, mesh=mesh, in_specs=in_specs, out_specs=out_specs, check_vma=False)
```

```python
import jax
import jax.numpy as jnp
from jax import lax
from jax.sharding import PartitionSpec as P
from jax.experimental import pallas as pl
from jax.experimental.pallas import tpu as pltpu

TILE = 128


step_size = 0.5
hop_kappa = 0.5
coupling = 0.25


def with_halo(block, sides, width):
    for axis, dim in sides:
        count = lax.axis_size(axis)
        forward = [(i, i + 1) for i in range(count - 1)]
        forward.append((count - 1, 0))
        backward = [(target, source) for source, target in forward]
        low = lax.ppermute(
            lax.slice_in_dim(block, block.shape[dim] - width, None, axis=dim), axis, forward
        )
        high = lax.ppermute(lax.slice_in_dim(block, 0, width, axis=dim), axis, backward)
        block = jnp.concatenate([low, block, high], axis=dim)
    return block


def from_behind(value, axis, steps):
    count = lax.axis_size(axis)
    pairs = [(source, (source + steps) % count) for source in range(count)]
    return lax.ppermute(value, axis, pairs)


def split_dot(a, b):
    a_hi = a.astype(jnp.bfloat16)
    a_lo = (a - a_hi.astype(jnp.float32)).astype(jnp.bfloat16)
    b_hi = b.astype(jnp.bfloat16)
    b_lo = (b - b_hi.astype(jnp.float32)).astype(jnp.bfloat16)

    def part(x, y):
        return jnp.dot(x, y, preferred_element_type=jnp.float32)

    return part(a_hi, b_hi) + (part(a_hi, b_lo) + part(a_lo, b_hi))


def substep(field, moment, got, tiles, pick, send_ids, scale, advance, send):
    slices, site_count = field.shape
    rows, kept = tiles.shape[0], tiles.shape[1] // TILE
    slots = send_ids.shape[0] * send_ids.shape[1]

    def kernel(pick_ref, sid_ref, f_ref, p_ref, got_ref, tiles_ref, *refs):
        outs = list(refs)
        p_out = outs.pop(0)
        f_out = outs.pop(0) if advance else None
        send_out = outs.pop(0) if send else None
        held = outs.pop(0) if send else None
        for r in range(rows):
            cols = slice(r * TILE, (r + 1) * TILE)
            pieces = [f_ref[:, cols]] + [got_ref[pick_ref[r, k]] for k in range(1, kept)]
            acc = split_dot(jnp.concatenate(pieces, axis=1), tiles_ref[r])
            p_new = p_ref[:, cols] - scale * acc
            p_out[:, cols] = p_new
            if advance:
                f_new = f_ref[:, cols] + step_size * p_new
                f_out[:, cols] = f_new
                if send:
                    held[r] = f_new
        if send:
            def copy_one(s, carry):
                send_out[s] = held[sid_ref[s // 2, s % 2]]
                return carry
            lax.fori_loop(0, slots, copy_one, 0)

    vmem = pl.BlockSpec(memory_space=pltpu.VMEM)
    smem = pl.BlockSpec(memory_space=pltpu.SMEM)
    out_shape = [jax.ShapeDtypeStruct(field.shape, jnp.float32)]
    if advance:
        out_shape.append(jax.ShapeDtypeStruct(field.shape, jnp.float32))
    scratch = []
    if send:
        out_shape.append(jax.ShapeDtypeStruct((slots, slices, TILE), jnp.float32))
        scratch.append(pltpu.VMEM((rows, slices, TILE), jnp.float32))
    return pl.pallas_call(
        kernel,
        out_shape=tuple(out_shape),
        in_specs=[smem, smem, vmem, vmem, vmem, vmem],
        out_specs=tuple([vmem] * len(out_shape)),
        scratch_shapes=scratch,
    )(pick, send_ids, field, moment, got, tiles)


def body(field, momentum, solution, tiles, columns, neighbours):
    slices = field.shape[0]
    tile_rows = tiles.shape[0]
    kept = tiles.shape[1]
    site_count = field.shape[1]
    space_count = lax.axis_size("space")
    me = lax.axis_index("space")

    run_of = columns // tile_rows
    local_id = columns % tile_rows
    remote = run_of != me
    runs = jnp.arange(space_count, dtype=jnp.int32)
    hit = remote[:, :, None] & (run_of[:, :, None] == runs[None, None, :])
    lo = jnp.min(jnp.where(hit, local_id[:, :, None], tile_rows), axis=(0, 1))
    hi = jnp.max(jnp.where(hit, local_id[:, :, None], -1), axis=(0, 1))
    lo = jnp.clip(lo, 0, tile_rows - 1)
    hi = jnp.clip(hi, 0, tile_rows - 1)
    request = jnp.stack([lo, hi], axis=1)
    send_ids = lax.all_to_all(request, "space", 0, 0)
    slot = jnp.where(local_id == lo[run_of], 0, 1)

    pick = jnp.where(remote, run_of * 2 + slot, 0)

    def exchange(sent):
        return lax.all_to_all(sent, "space", 0, 0, tiled=True)

    tiles = tiles.transpose(0, 1, 3, 2).reshape(tile_rows, kept * TILE, TILE)
    total_sites = site_count * space_count
    first_site = me * site_count
    lookup = (neighbours - first_site + TILE) % total_sites
    parity_sign = jnp.where(lax.axis_index("tm") == 0, -1.0, 1.0).astype(jnp.float32)
    widened = with_halo(solution, (("space", 1),), TILE)
    blocks = site_count // TILE
    starts = (jnp.arange(blocks, dtype=jnp.int32) * TILE)[:, None, None]
    offsets = lookup.reshape(3, blocks, TILE).transpose(1, 0, 2) - starts
    window = jnp.arange(3 * TILE, dtype=jnp.int32)[None, None, :, None]
    adjacency = jnp.sum((offsets[:, :, None, :] == window).astype(jnp.float32), axis=1)
    parts = widened.reshape(slices, blocks + 2, TILE)
    windows = jnp.concatenate([parts[:, :-2], parts[:, 1:-1], parts[:, 2:]], axis=2)
    beside = jnp.einsum("tbj,bji->tbi", windows, adjacency, precision=lax.Precision.HIGHEST)
    hopped = solution + hop_kappa * beside.reshape(slices, site_count)
    own = field.reshape(slices, tile_rows, TILE)
    first = jnp.take(own, send_ids.reshape(-1), axis=1, mode="clip").transpose(1, 0, 2)
    got = exchange(first)
    moment, field_one, sent = substep(field, momentum, got, tiles, pick, send_ids, 0.5 * step_size, True, True)
    arrived = from_behind(hopped[-1:], "tm", 1)
    got = exchange(sent)
    moment, field_two, sent = substep(field_one, moment, got, tiles, pick, send_ids, step_size, True, True)
    sent, arrived = lax.optimization_barrier((sent, arrived))
    got = exchange(sent)
    (moment,) = substep(field_two, moment, got, tiles, pick, send_ids, 0.5 * step_size, False, False)

    earlier = jnp.concatenate([parity_sign * arrived, hopped[:-1]], axis=0)
    link_factor = jnp.exp(coupling * field_two)
    shifted = solution - link_factor * earlier
    force = 2.0 * coupling * shifted * link_factor * earlier
    return (field_two, moment, force)


def solution(mesh):
    in_specs = (
        P("tm", "space"),
        P("tm", "space"),
        P("tm", "space"),
        P("space", None, None, None),
        P("space", None),
        P(None, "space"),
    )
    out_specs = (P("tm", "space"), P("tm", "space"), P("tm", "space"))
    return jax.shard_map(body, mesh=mesh, in_specs=in_specs, out_specs=out_specs, check_vma=False)
```

```python
import jax
import jax.numpy as jnp
from jax import lax
from jax.sharding import PartitionSpec as P
from jax.experimental import pallas as pl
from jax.experimental.pallas import tpu as pltpu

TILE = 128


step_size = 0.5
hop_kappa = 0.5
coupling = 0.25


def with_halo(block, sides, width):
    for axis, dim in sides:
        count = lax.axis_size(axis)
        forward = [(i, i + 1) for i in range(count - 1)]
        forward.append((count - 1, 0))
        backward = [(target, source) for source, target in forward]
        low = lax.ppermute(
            lax.slice_in_dim(block, block.shape[dim] - width, None, axis=dim), axis, forward
        )
        high = lax.ppermute(lax.slice_in_dim(block, 0, width, axis=dim), axis, backward)
        block = jnp.concatenate([low, block, high], axis=dim)
    return block


def from_behind(value, axis, steps):
    count = lax.axis_size(axis)
    pairs = [(source, (source + steps) % count) for source in range(count)]
    return lax.ppermute(value, axis, pairs)


def split_dot(a, b):
    a_hi = a.astype(jnp.bfloat16)
    a_lo = (a - a_hi.astype(jnp.float32)).astype(jnp.bfloat16)
    b_hi = b.astype(jnp.bfloat16)
    b_lo = (b - b_hi.astype(jnp.float32)).astype(jnp.bfloat16)

    def part(x, y):
        return jnp.dot(x, y, preferred_element_type=jnp.float32)

    return part(a_hi, b_hi) + (part(a_hi, b_lo) + part(a_lo, b_hi))


def substep(field, moment, got, tiles, pick, send_ids, scale, advance, send):
    slices, site_count = field.shape
    rows, kept = tiles.shape[0], tiles.shape[1] // TILE
    slots = send_ids.shape[0] * send_ids.shape[1]

    def kernel(pick_ref, sid_ref, f_ref, p_ref, got_ref, tiles_ref, *refs):
        outs = list(refs)
        p_out = outs.pop(0)
        f_out = outs.pop(0) if advance else None
        send_out = outs.pop(0) if send else None
        held = outs.pop(0) if send else None
        for r in range(rows):
            cols = slice(r * TILE, (r + 1) * TILE)
            pieces = [f_ref[:, cols]] + [got_ref[pick_ref[r, k]] for k in range(1, kept)]
            acc = split_dot(jnp.concatenate(pieces, axis=1), tiles_ref[r])
            p_new = p_ref[:, cols] - scale * acc
            p_out[:, cols] = p_new
            if advance:
                f_new = f_ref[:, cols] + step_size * p_new
                f_out[:, cols] = f_new
                if send:
                    held[r] = f_new
        if send:
            def copy_one(s, carry):
                send_out[s] = held[sid_ref[s // 2, s % 2]]
                return carry
            lax.fori_loop(0, slots, copy_one, 0)

    vmem = pl.BlockSpec(memory_space=pltpu.VMEM)
    smem = pl.BlockSpec(memory_space=pltpu.SMEM)
    out_shape = [jax.ShapeDtypeStruct(field.shape, jnp.float32)]
    if advance:
        out_shape.append(jax.ShapeDtypeStruct(field.shape, jnp.float32))
    scratch = []
    if send:
        out_shape.append(jax.ShapeDtypeStruct((slots, slices, TILE), jnp.float32))
        scratch.append(pltpu.VMEM((rows, slices, TILE), jnp.float32))
    return pl.pallas_call(
        kernel,
        out_shape=tuple(out_shape),
        in_specs=[smem, smem, vmem, vmem, vmem, vmem],
        out_specs=tuple([vmem] * len(out_shape)),
        scratch_shapes=scratch,
    )(pick, send_ids, field, moment, got, tiles)


def body(field, momentum, solution, tiles, columns, neighbours):
    slices = field.shape[0]
    tile_rows = tiles.shape[0]
    kept = tiles.shape[1]
    site_count = field.shape[1]
    space_count = lax.axis_size("space")
    me = lax.axis_index("space")

    run_of = columns // tile_rows
    local_id = columns % tile_rows
    remote = run_of != me
    runs = lax.broadcasted_iota(jnp.int32, (space_count, tile_rows * kept), 0)
    flat_run = jnp.where(remote, run_of, -1).reshape(1, -1)
    flat_id = local_id.reshape(1, -1)
    hit = flat_run == runs
    lo = jnp.min(jnp.where(hit, flat_id, tile_rows), axis=1)
    hi = jnp.max(jnp.where(hit, flat_id, -1), axis=1)
    lo = jnp.clip(lo, 0, tile_rows - 1)
    hi = jnp.clip(hi, 0, tile_rows - 1)
    lane = lax.broadcasted_iota(jnp.int32, (space_count, TILE), 1)
    request = jnp.where(lane == 0, lo[:, None], jnp.where(lane == 1, hi[:, None], 0))
    send_ids = lax.all_to_all(request, "space", 0, 0, tiled=True)[:, :2]
    slot = jnp.where(local_id == lo[run_of], 0, 1)

    pick = jnp.where(remote, run_of * 2 + slot, 0)

    def exchange(sent):
        return lax.all_to_all(sent, "space", 0, 0, tiled=True)

    tiles = tiles.transpose(0, 1, 3, 2).reshape(tile_rows, kept * TILE, TILE)
    total_sites = site_count * space_count
    first_site = me * site_count
    lookup = (neighbours - first_site + TILE) % total_sites
    parity_sign = jnp.where(lax.axis_index("tm") == 0, -1.0, 1.0).astype(jnp.float32)
    widened = with_halo(solution, (("space", 1),), TILE)
    blocks = site_count // TILE
    starts = (jnp.arange(blocks, dtype=jnp.int32) * TILE)[:, None, None]
    offsets = lookup.reshape(3, blocks, TILE).transpose(1, 0, 2) - starts
    window = jnp.arange(3 * TILE, dtype=jnp.int32)[None, None, :, None]
    adjacency = jnp.sum((offsets[:, :, None, :] == window).astype(jnp.float32), axis=1)
    parts = widened.reshape(slices, blocks + 2, TILE)
    windows = jnp.concatenate([parts[:, :-2], parts[:, 1:-1], parts[:, 2:]], axis=2)
    beside = jnp.einsum("tbj,bji->tbi", windows, adjacency, precision=lax.Precision.HIGHEST)
    hopped = solution + hop_kappa * beside.reshape(slices, site_count)
    own = field.reshape(slices, tile_rows, TILE)
    first = jnp.take(own, send_ids.reshape(-1), axis=1, mode="clip").transpose(1, 0, 2)
    got = exchange(first)
    moment, field_one, sent = substep(field, momentum, got, tiles, pick, send_ids, 0.5 * step_size, True, True)
    arrived = from_behind(hopped[-1:], "tm", 1)
    got = exchange(sent)
    moment, field_two, sent = substep(field_one, moment, got, tiles, pick, send_ids, step_size, True, True)
    sent, arrived = lax.optimization_barrier((sent, arrived))
    got = exchange(sent)
    (moment,) = substep(field_two, moment, got, tiles, pick, send_ids, 0.5 * step_size, False, False)

    earlier = jnp.concatenate([parity_sign * arrived, hopped[:-1]], axis=0)
    link_factor = jnp.exp(coupling * field_two)
    shifted = solution - link_factor * earlier
    force = 2.0 * coupling * shifted * link_factor * earlier
    return (field_two, moment, force)


def solution(mesh):
    in_specs = (
        P("tm", "space"),
        P("tm", "space"),
        P("tm", "space"),
        P("space", None, None, None),
        P("space", None),
        P(None, "space"),
    )
    out_specs = (P("tm", "space"), P("tm", "space"), P("tm", "space"))
    return jax.shard_map(body, mesh=mesh, in_specs=in_specs, out_specs=out_specs, check_vma=False)
```

```python
import jax
import jax.numpy as jnp
from jax import lax
from jax.sharding import PartitionSpec as P
from jax.experimental import pallas as pl
from jax.experimental.pallas import tpu as pltpu

TILE = 128


step_size = 0.5
hop_kappa = 0.5
coupling = 0.25


def with_halo(block, sides, width):
    for axis, dim in sides:
        count = lax.axis_size(axis)
        forward = [(i, i + 1) for i in range(count - 1)]
        forward.append((count - 1, 0))
        backward = [(target, source) for source, target in forward]
        low = lax.ppermute(
            lax.slice_in_dim(block, block.shape[dim] - width, None, axis=dim), axis, forward
        )
        high = lax.ppermute(lax.slice_in_dim(block, 0, width, axis=dim), axis, backward)
        block = jnp.concatenate([low, block, high], axis=dim)
    return block


def from_behind(value, axis, steps):
    count = lax.axis_size(axis)
    pairs = [(source, (source + steps) % count) for source in range(count)]
    return lax.ppermute(value, axis, pairs)


def split_dot(a, b):
    a_hi = a.astype(jnp.bfloat16)
    a_lo = (a - a_hi.astype(jnp.float32)).astype(jnp.bfloat16)
    b_hi = b.astype(jnp.bfloat16)
    b_lo = (b - b_hi.astype(jnp.float32)).astype(jnp.bfloat16)

    def part(x, y):
        return jnp.dot(x, y, preferred_element_type=jnp.float32)

    return part(a_hi, b_hi) + (part(a_hi, b_lo) + part(a_lo, b_hi))


def substep(field, moment, got, tiles, pick, send_ids, scale, advance, send):
    slices, site_count = field.shape
    rows, kept = tiles.shape[0], tiles.shape[1] // TILE
    slots = send_ids.shape[0] * send_ids.shape[1]

    def kernel(pick_ref, sid_ref, f_ref, p_ref, got_ref, tiles_ref, *refs):
        outs = list(refs)
        p_out = outs.pop(0)
        f_out = outs.pop(0) if advance else None
        send_out = outs.pop(0) if send else None
        held = outs.pop(0) if send else None
        for r in range(rows):
            cols = slice(r * TILE, (r + 1) * TILE)
            pieces = [f_ref[:, cols]] + [got_ref[pick_ref[r, k]] for k in range(1, kept)]
            acc = split_dot(jnp.concatenate(pieces, axis=1), tiles_ref[r])
            p_new = p_ref[:, cols] - scale * acc
            p_out[:, cols] = p_new
            if advance:
                f_new = f_ref[:, cols] + step_size * p_new
                f_out[:, cols] = f_new
                if send:
                    held[r] = f_new
        if send:
            pair = sid_ref.shape[1]
            for s in range(slots):
                send_out[s] = held[sid_ref[s // pair, s % pair]]

    vmem = pl.BlockSpec(memory_space=pltpu.VMEM)
    smem = pl.BlockSpec(memory_space=pltpu.SMEM)
    out_shape = [jax.ShapeDtypeStruct(field.shape, jnp.float32)]
    if advance:
        out_shape.append(jax.ShapeDtypeStruct(field.shape, jnp.float32))
    scratch = []
    if send:
        out_shape.append(jax.ShapeDtypeStruct((slots, slices, TILE), jnp.float32))
        scratch.append(pltpu.VMEM((rows, slices, TILE), jnp.float32))
    return pl.pallas_call(
        kernel,
        out_shape=tuple(out_shape),
        in_specs=[smem, smem, vmem, vmem, vmem, vmem],
        out_specs=tuple([vmem] * len(out_shape)),
        scratch_shapes=scratch,
    )(pick, send_ids, field, moment, got, tiles)


def body(field, momentum, solution, tiles, columns, neighbours):
    slices = field.shape[0]
    tile_rows = tiles.shape[0]
    kept = tiles.shape[1]
    site_count = field.shape[1]
    space_count = lax.axis_size("space")
    me = lax.axis_index("space")

    run_of = lax.div(columns, tile_rows)
    local_id = lax.rem(columns, tile_rows)
    remote = run_of != me
    runs = lax.broadcasted_iota(jnp.int32, (space_count, tile_rows * kept), 0)
    flat_run = jnp.where(remote, run_of, -1).reshape(1, -1)
    flat_id = local_id.reshape(1, -1)
    hit = flat_run == runs
    lo = jnp.min(jnp.where(hit, flat_id, tile_rows), axis=1)
    hi = jnp.max(jnp.where(hit, flat_id, -1), axis=1)
    lo = jnp.clip(lo, 0, tile_rows - 1)
    hi = jnp.clip(hi, 0, tile_rows - 1)
    lane = lax.broadcasted_iota(jnp.int32, (space_count, TILE), 1)
    request = jnp.where(lane == 0, lo[:, None], jnp.where(lane == 1, hi[:, None], 0))
    send_ids = lax.all_to_all(request, "space", 0, 0, tiled=True)[:, :2]
    slot = jnp.where(local_id == lo[run_of], 0, 1)

    pick = jnp.where(remote, run_of * 2 + slot, 0)

    def exchange(sent):
        return lax.all_to_all(sent, "space", 0, 0, tiled=True)

    tiles = tiles.transpose(0, 1, 3, 2).reshape(tile_rows, kept * TILE, TILE)
    total_sites = site_count * space_count
    first_site = me * site_count
    lookup = (neighbours - first_site + TILE) % total_sites
    parity_sign = jnp.where(lax.axis_index("tm") == 0, -1.0, 1.0).astype(jnp.float32)
    widened = with_halo(solution, (("space", 1),), TILE)
    blocks = site_count // TILE
    starts = (jnp.arange(blocks, dtype=jnp.int32) * TILE)[:, None, None]
    offsets = lookup.reshape(3, blocks, TILE).transpose(1, 0, 2) - starts
    window = jnp.arange(3 * TILE, dtype=jnp.int32)[None, None, :, None]
    adjacency = jnp.sum((offsets[:, :, None, :] == window).astype(jnp.float32), axis=1)
    parts = widened.reshape(slices, blocks + 2, TILE)
    windows = jnp.concatenate([parts[:, :-2], parts[:, 1:-1], parts[:, 2:]], axis=2)
    beside = jnp.einsum("tbj,bji->tbi", windows, adjacency, precision=lax.Precision.HIGHEST)
    hopped = solution + hop_kappa * beside.reshape(slices, site_count)
    own = field.reshape(slices, tile_rows, TILE)
    first = jnp.take(own, send_ids.reshape(-1), axis=1, mode="clip").transpose(1, 0, 2)
    got = exchange(first)
    moment, field_one, sent = substep(field, momentum, got, tiles, pick, send_ids, 0.5 * step_size, True, True)
    arrived = from_behind(hopped[-1:], "tm", 1)
    got = exchange(sent)
    moment, field_two, sent = substep(field_one, moment, got, tiles, pick, send_ids, step_size, True, True)
    sent, arrived = lax.optimization_barrier((sent, arrived))
    got = exchange(sent)
    (moment,) = substep(field_two, moment, got, tiles, pick, send_ids, 0.5 * step_size, False, False)

    earlier = jnp.concatenate([parity_sign * arrived, hopped[:-1]], axis=0)
    link_factor = jnp.exp(coupling * field_two)
    shifted = solution - link_factor * earlier
    force = 2.0 * coupling * shifted * link_factor * earlier
    return (field_two, moment, force)


def solution(mesh):
    in_specs = (
        P("tm", "space"),
        P("tm", "space"),
        P("tm", "space"),
        P("space", None, None, None),
        P("space", None),
        P(None, "space"),
    )
    out_specs = (P("tm", "space"), P("tm", "space"), P("tm", "space"))
    return jax.shard_map(body, mesh=mesh, in_specs=in_specs, out_specs=out_specs, check_vma=False)
```

```python
import jax
import jax.numpy as jnp
from jax import lax
from jax.sharding import PartitionSpec as P
from jax.experimental import pallas as pl
from jax.experimental.pallas import tpu as pltpu

TILE = 128


step_size = 0.5
hop_kappa = 0.5
coupling = 0.25


def with_halo(block, sides, width):
    for axis, dim in sides:
        count = lax.axis_size(axis)
        forward = [(i, i + 1) for i in range(count - 1)]
        forward.append((count - 1, 0))
        backward = [(target, source) for source, target in forward]
        low = lax.ppermute(
            lax.slice_in_dim(block, block.shape[dim] - width, None, axis=dim), axis, forward
        )
        high = lax.ppermute(lax.slice_in_dim(block, 0, width, axis=dim), axis, backward)
        block = jnp.concatenate([low, block, high], axis=dim)
    return block


def from_behind(value, axis, steps):
    count = lax.axis_size(axis)
    pairs = [(source, (source + steps) % count) for source in range(count)]
    return lax.ppermute(value, axis, pairs)


def split_dot(a, b):
    a_hi = a.astype(jnp.bfloat16)
    a_lo = (a - a_hi.astype(jnp.float32)).astype(jnp.bfloat16)
    b_hi = b.astype(jnp.bfloat16)
    b_lo = (b - b_hi.astype(jnp.float32)).astype(jnp.bfloat16)

    def part(x, y):
        return jnp.dot(x, y, preferred_element_type=jnp.float32)

    return part(a_hi, b_hi) + (part(a_hi, b_lo) + part(a_lo, b_hi))


def substep(field, moment, local, got, tiles, pick, send_ids, scale, advance, send):
    slices, site_count = field.shape
    rows, kept = tiles.shape[0], tiles.shape[1] // TILE + 1
    slots = send_ids.shape[0] * send_ids.shape[1]

    def kernel(pick_ref, sid_ref, f_ref, p_ref, local_ref, got_ref, tiles_ref, *refs):
        outs = list(refs)
        p_out = outs.pop(0)
        f_out = outs.pop(0) if advance else None
        send_out = outs.pop(0) if send else None
        held = outs.pop(0) if send else None
        for r in range(rows):
            cols = slice(r * TILE, (r + 1) * TILE)
            pieces = [got_ref[pick_ref[r, k]] for k in range(1, kept)]
            acc = local_ref[:, cols] + split_dot(jnp.concatenate(pieces, axis=1), tiles_ref[r])
            p_new = p_ref[:, cols] - scale * acc
            p_out[:, cols] = p_new
            if advance:
                f_new = f_ref[:, cols] + step_size * p_new
                f_out[:, cols] = f_new
                if send:
                    held[r] = f_new
        if send:
            pair = sid_ref.shape[1]
            for s in range(slots):
                send_out[s] = held[sid_ref[s // pair, s % pair]]

    vmem = pl.BlockSpec(memory_space=pltpu.VMEM)
    smem = pl.BlockSpec(memory_space=pltpu.SMEM)
    out_shape = [jax.ShapeDtypeStruct(field.shape, jnp.float32)]
    if advance:
        out_shape.append(jax.ShapeDtypeStruct(field.shape, jnp.float32))
    scratch = []
    if send:
        out_shape.append(jax.ShapeDtypeStruct((slots, slices, TILE), jnp.float32))
        scratch.append(pltpu.VMEM((rows, slices, TILE), jnp.float32))
    return pl.pallas_call(
        kernel,
        out_shape=tuple(out_shape),
        in_specs=[smem, smem, vmem, vmem, vmem, vmem, vmem],
        out_specs=tuple([vmem] * len(out_shape)),
        scratch_shapes=scratch,
    )(pick, send_ids, field, moment, local, got, tiles)


def body(field, momentum, solution, tiles, columns, neighbours):
    slices = field.shape[0]
    tile_rows = tiles.shape[0]
    kept = tiles.shape[1]
    site_count = field.shape[1]
    space_count = lax.axis_size("space")
    me = lax.axis_index("space")

    run_of = lax.div(columns, tile_rows)
    local_id = lax.rem(columns, tile_rows)
    remote = run_of != me
    runs = lax.broadcasted_iota(jnp.int32, (space_count, tile_rows * kept), 0)
    flat_run = jnp.where(remote, run_of, -1).reshape(1, -1)
    flat_id = local_id.reshape(1, -1)
    hit = flat_run == runs
    lo = jnp.min(jnp.where(hit, flat_id, tile_rows), axis=1)
    hi = jnp.max(jnp.where(hit, flat_id, -1), axis=1)
    lo = jnp.clip(lo, 0, tile_rows - 1)
    hi = jnp.clip(hi, 0, tile_rows - 1)
    lane = lax.broadcasted_iota(jnp.int32, (space_count, TILE), 1)
    request = jnp.where(lane == 0, lo[:, None], jnp.where(lane == 1, hi[:, None], 0))
    send_ids = lax.all_to_all(request, "space", 0, 0, tiled=True)[:, :2]
    slot = jnp.where(local_id == lo[run_of], 0, 1)

    pick = jnp.where(remote, run_of * 2 + slot, 0)

    def exchange(sent):
        return lax.all_to_all(sent, "space", 0, 0, tiled=True)

    own_tiles = tiles[:, 0]
    tiles = tiles[:, 1:].transpose(0, 1, 3, 2).reshape(tile_rows, (kept - 1) * TILE, TILE)

    def local_term(values):
        blocks = values.reshape(slices, tile_rows, TILE)
        mixed = jnp.einsum("rij,trj->tri", own_tiles, blocks, precision=lax.Precision.HIGHEST)
        return mixed.reshape(slices, site_count)

    total_sites = site_count * space_count
    first_site = me * site_count
    lookup = (neighbours - first_site + TILE) % total_sites
    parity_sign = jnp.where(lax.axis_index("tm") == 0, -1.0, 1.0).astype(jnp.float32)
    widened = with_halo(solution, (("space", 1),), TILE)
    blocks = site_count // TILE
    starts = (jnp.arange(blocks, dtype=jnp.int32) * TILE)[:, None, None]
    offsets = lookup.reshape(3, blocks, TILE).transpose(1, 0, 2) - starts
    window = jnp.arange(3 * TILE, dtype=jnp.int32)[None, None, :, None]
    adjacency = jnp.sum((offsets[:, :, None, :] == window).astype(jnp.float32), axis=1)
    parts = widened.reshape(slices, blocks + 2, TILE)
    windows = jnp.concatenate([parts[:, :-2], parts[:, 1:-1], parts[:, 2:]], axis=2)
    beside = jnp.einsum("tbj,bji->tbi", windows, adjacency, precision=lax.Precision.HIGHEST)
    hopped = solution + hop_kappa * beside.reshape(slices, site_count)
    own = field.reshape(slices, tile_rows, TILE)
    first = jnp.take(own, send_ids.reshape(-1), axis=1, mode="clip").transpose(1, 0, 2)
    got = exchange(first)
    moment, field_one, sent = substep(field, momentum, local_term(field), got, tiles, pick, send_ids, 0.5 * step_size, True, True)
    arrived = from_behind(hopped[-1:], "tm", 1)
    got = exchange(sent)
    moment, field_two, sent = substep(field_one, moment, local_term(field_one), got, tiles, pick, send_ids, step_size, True, True)
    sent, arrived = lax.optimization_barrier((sent, arrived))
    got = exchange(sent)
    (moment,) = substep(field_two, moment, local_term(field_two), got, tiles, pick, send_ids, 0.5 * step_size, False, False)

    earlier = jnp.concatenate([parity_sign * arrived, hopped[:-1]], axis=0)
    link_factor = jnp.exp(coupling * field_two)
    shifted = solution - link_factor * earlier
    force = 2.0 * coupling * shifted * link_factor * earlier
    return (field_two, moment, force)


def solution(mesh):
    in_specs = (
        P("tm", "space"),
        P("tm", "space"),
        P("tm", "space"),
        P("space", None, None, None),
        P("space", None),
        P(None, "space"),
    )
    out_specs = (P("tm", "space"), P("tm", "space"), P("tm", "space"))
    return jax.shard_map(body, mesh=mesh, in_specs=in_specs, out_specs=out_specs, check_vma=False)
```

```python
import jax
import jax.numpy as jnp
from jax import lax
from jax.sharding import PartitionSpec as P
from jax.experimental import pallas as pl
from jax.experimental.pallas import tpu as pltpu

TILE = 128


step_size = 0.5
hop_kappa = 0.5
coupling = 0.25


def with_halo(block, sides, width):
    for axis, dim in sides:
        count = lax.axis_size(axis)
        forward = [(i, i + 1) for i in range(count - 1)]
        forward.append((count - 1, 0))
        backward = [(target, source) for source, target in forward]
        low = lax.ppermute(
            lax.slice_in_dim(block, block.shape[dim] - width, None, axis=dim), axis, forward
        )
        high = lax.ppermute(lax.slice_in_dim(block, 0, width, axis=dim), axis, backward)
        block = jnp.concatenate([low, block, high], axis=dim)
    return block


def from_behind(value, axis, steps):
    count = lax.axis_size(axis)
    pairs = [(source, (source + steps) % count) for source in range(count)]
    return lax.ppermute(value, axis, pairs)


def split_dot(a, b):
    a_hi = a.astype(jnp.bfloat16)
    a_lo = (a - a_hi.astype(jnp.float32)).astype(jnp.bfloat16)
    b_hi = b.astype(jnp.bfloat16)
    b_lo = (b - b_hi.astype(jnp.float32)).astype(jnp.bfloat16)

    def part(x, y):
        return jnp.dot(x, y, preferred_element_type=jnp.float32)

    return part(a_hi, b_hi) + (part(a_hi, b_lo) + part(a_lo, b_hi))


def substep(field, moment, got, tiles, pick, send_ids, scale, advance, send):
    slices, site_count = field.shape
    rows, kept = tiles.shape[0], tiles.shape[1] // TILE
    slots = send_ids.shape[0] * send_ids.shape[1]

    def kernel(pick_ref, sid_ref, f_ref, p_ref, got_ref, tiles_ref, *refs):
        outs = list(refs)
        p_out = outs.pop(0)
        f_out = outs.pop(0) if advance else None
        send_out = outs.pop(0) if send else None
        held = outs.pop(0) if send else None
        for r in range(rows):
            cols = slice(r * TILE, (r + 1) * TILE)
            pieces = [f_ref[:, cols]] + [got_ref[pick_ref[r, k]] for k in range(1, kept)]
            acc = split_dot(jnp.concatenate(pieces, axis=1), tiles_ref[r])
            p_new = p_ref[:, cols] - scale * acc
            p_out[:, cols] = p_new
            if advance:
                f_new = f_ref[:, cols] + step_size * p_new
                f_out[:, cols] = f_new
                if send:
                    held[r] = f_new
        if send:
            pair = sid_ref.shape[1]
            for s in range(slots):
                send_out[s] = held[sid_ref[s // pair, s % pair]]

    vmem = pl.BlockSpec(memory_space=pltpu.VMEM)
    smem = pl.BlockSpec(memory_space=pltpu.SMEM)
    out_shape = [jax.ShapeDtypeStruct(field.shape, jnp.float32)]
    if advance:
        out_shape.append(jax.ShapeDtypeStruct(field.shape, jnp.float32))
    scratch = []
    if send:
        out_shape.append(jax.ShapeDtypeStruct((slots, slices, TILE), jnp.float32))
        scratch.append(pltpu.VMEM((rows, slices, TILE), jnp.float32))
    return pl.pallas_call(
        kernel,
        out_shape=tuple(out_shape),
        in_specs=[smem, smem, vmem, vmem, vmem, vmem],
        out_specs=tuple([vmem] * len(out_shape)),
        scratch_shapes=scratch,
    )(pick, send_ids, field, moment, got, tiles)


def body(field, momentum, solution, tiles, columns, neighbours):
    slices = field.shape[0]
    tile_rows = tiles.shape[0]
    kept = tiles.shape[1]
    site_count = field.shape[1]
    space_count = lax.axis_size("space")
    me = lax.axis_index("space")

    run_of = lax.div(columns, tile_rows)
    local_id = lax.rem(columns, tile_rows)
    remote = run_of != me
    runs = lax.broadcasted_iota(jnp.int32, (space_count, tile_rows * kept), 0)
    flat = columns.reshape(1, -1)
    flat_run = lax.div(flat, tile_rows)
    flat_id = lax.rem(flat, tile_rows)
    hit = (flat_run == runs) & (flat_run != me)
    lo = jnp.min(jnp.where(hit, flat_id, tile_rows), axis=1)
    hi = jnp.max(jnp.where(hit, flat_id, -1), axis=1)
    lo = jnp.clip(lo, 0, tile_rows - 1)
    hi = jnp.clip(hi, 0, tile_rows - 1)
    lane = lax.broadcasted_iota(jnp.int32, (space_count, TILE), 1)
    request = jnp.where(lane == 0, lo[:, None], jnp.where(lane == 1, hi[:, None], 0))
    send_ids = lax.all_to_all(request, "space", 0, 0, tiled=True)[:, :2]
    slot = jnp.where(local_id == lo[run_of], 0, 1)

    pick = jnp.where(remote, run_of * 2 + slot, 0)

    def exchange(sent):
        return lax.all_to_all(sent, "space", 0, 0, tiled=True)

    tiles = tiles.transpose(0, 1, 3, 2).reshape(tile_rows, kept * TILE, TILE)
    total_sites = site_count * space_count
    first_site = me * site_count
    lookup = (neighbours - first_site + TILE) % total_sites
    parity_sign = jnp.where(lax.axis_index("tm") == 0, -1.0, 1.0).astype(jnp.float32)
    widened = with_halo(solution, (("space", 1),), TILE)
    blocks = site_count // TILE
    starts = (jnp.arange(blocks, dtype=jnp.int32) * TILE)[:, None, None]
    offsets = lookup.reshape(3, blocks, TILE).transpose(1, 0, 2) - starts
    window = jnp.arange(3 * TILE, dtype=jnp.int32)[None, None, :, None]
    adjacency = jnp.sum((offsets[:, :, None, :] == window).astype(jnp.float32), axis=1)
    parts = widened.reshape(slices, blocks + 2, TILE)
    windows = jnp.concatenate([parts[:, :-2], parts[:, 1:-1], parts[:, 2:]], axis=2)
    beside = jnp.einsum("tbj,bji->tbi", windows, adjacency, precision=lax.Precision.HIGHEST)
    hopped = solution + hop_kappa * beside.reshape(slices, site_count)
    own = field.reshape(slices, tile_rows, TILE)
    first = jnp.take(own, send_ids.reshape(-1), axis=1, mode="clip").transpose(1, 0, 2)
    got = exchange(first)
    moment, field_one, sent = substep(field, momentum, got, tiles, pick, send_ids, 0.5 * step_size, True, True)
    arrived = from_behind(hopped[-1:], "tm", 1)
    got = exchange(sent)
    moment, field_two, sent = substep(field_one, moment, got, tiles, pick, send_ids, step_size, True, True)
    sent, arrived = lax.optimization_barrier((sent, arrived))
    got = exchange(sent)
    (moment,) = substep(field_two, moment, got, tiles, pick, send_ids, 0.5 * step_size, False, False)

    earlier = jnp.concatenate([parity_sign * arrived, hopped[:-1]], axis=0)
    link_factor = jnp.exp(coupling * field_two)
    shifted = solution - link_factor * earlier
    force = 2.0 * coupling * shifted * link_factor * earlier
    return (field_two, moment, force)


def solution(mesh):
    in_specs = (
        P("tm", "space"),
        P("tm", "space"),
        P("tm", "space"),
        P("space", None, None, None),
        P("space", None),
        P(None, "space"),
    )
    out_specs = (P("tm", "space"), P("tm", "space"), P("tm", "space"))
    return jax.shard_map(body, mesh=mesh, in_specs=in_specs, out_specs=out_specs, check_vma=False)
```

```python
import jax
import jax.numpy as jnp
from jax import lax
from jax.sharding import PartitionSpec as P
from jax.experimental import pallas as pl
from jax.experimental.pallas import tpu as pltpu

TILE = 128


step_size = 0.5
hop_kappa = 0.5
coupling = 0.25


def with_halo(block, sides, width):
    for axis, dim in sides:
        count = lax.axis_size(axis)
        forward = [(i, i + 1) for i in range(count - 1)]
        forward.append((count - 1, 0))
        backward = [(target, source) for source, target in forward]
        low = lax.ppermute(
            lax.slice_in_dim(block, block.shape[dim] - width, None, axis=dim), axis, forward
        )
        high = lax.ppermute(lax.slice_in_dim(block, 0, width, axis=dim), axis, backward)
        block = jnp.concatenate([low, block, high], axis=dim)
    return block


def from_behind(value, axis, steps):
    count = lax.axis_size(axis)
    pairs = [(source, (source + steps) % count) for source in range(count)]
    return lax.ppermute(value, axis, pairs)


def split_dot(a, b):
    a_hi = a.astype(jnp.bfloat16)
    a_lo = (a - a_hi.astype(jnp.float32)).astype(jnp.bfloat16)
    b_hi = b.astype(jnp.bfloat16)
    b_lo = (b - b_hi.astype(jnp.float32)).astype(jnp.bfloat16)

    def part(x, y):
        return jnp.dot(x, y, preferred_element_type=jnp.float32)

    return part(a_hi, b_hi) + (part(a_hi, b_lo) + part(a_lo, b_hi))


def substep(field, moment, got, tiles, pick, send_ids, scale, advance, send):
    slices, site_count = field.shape
    rows, kept = tiles.shape[0], tiles.shape[1] // TILE
    slots = send_ids.shape[0] * send_ids.shape[1]

    def kernel(pick_ref, sid_ref, f_ref, p_ref, got_ref, tiles_ref, *refs):
        outs = list(refs)
        p_out = outs.pop(0)
        f_out = outs.pop(0) if advance else None
        send_out = outs.pop(0) if send else None
        held = outs.pop(0) if send else None
        for r in range(rows):
            cols = slice(r * TILE, (r + 1) * TILE)
            pieces = [f_ref[:, cols]] + [got_ref[pick_ref[r, k]] for k in range(1, kept)]
            acc = split_dot(jnp.concatenate(pieces, axis=1), tiles_ref[r])
            p_new = p_ref[:, cols] - scale * acc
            p_out[:, cols] = p_new
            if advance:
                f_new = f_ref[:, cols] + step_size * p_new
                f_out[:, cols] = f_new
                if send:
                    held[r] = f_new
        if send:
            pair = sid_ref.shape[1]
            for s in range(slots):
                send_out[s] = held[sid_ref[s // pair, s % pair]]

    vmem = pl.BlockSpec(memory_space=pltpu.VMEM)
    smem = pl.BlockSpec(memory_space=pltpu.SMEM)
    out_shape = [jax.ShapeDtypeStruct(field.shape, jnp.float32)]
    if advance:
        out_shape.append(jax.ShapeDtypeStruct(field.shape, jnp.float32))
    scratch = []
    if send:
        out_shape.append(jax.ShapeDtypeStruct((slots, slices, TILE), jnp.float32))
        scratch.append(pltpu.VMEM((rows, slices, TILE), jnp.float32))
    return pl.pallas_call(
        kernel,
        out_shape=tuple(out_shape),
        in_specs=[smem, smem, vmem, vmem, vmem, vmem],
        out_specs=tuple([vmem] * len(out_shape)),
        scratch_shapes=scratch,
    )(pick, send_ids, field, moment, got, tiles)


def body(field, momentum, solution, tiles, columns, neighbours):
    slices = field.shape[0]
    tile_rows = tiles.shape[0]
    kept = tiles.shape[1]
    site_count = field.shape[1]
    space_count = lax.axis_size("space")
    me = lax.axis_index("space")

    run_of = lax.div(columns, tile_rows)
    local_id = lax.rem(columns, tile_rows)
    remote = run_of != me
    runs = lax.broadcasted_iota(jnp.int32, (space_count, tile_rows * kept), 0)
    flat_run = jnp.where(remote, run_of, -1).reshape(1, -1)
    flat_id = local_id.reshape(1, -1)
    hit = flat_run == runs
    lo = jnp.min(jnp.where(hit, flat_id, tile_rows), axis=1)
    hi = jnp.max(jnp.where(hit, flat_id, -1), axis=1)
    lo = jnp.clip(lo, 0, tile_rows - 1)
    hi = jnp.clip(hi, 0, tile_rows - 1)
    lane = lax.broadcasted_iota(jnp.int32, (space_count, TILE), 1)
    request = jnp.where(lane == 0, lo[:, None], jnp.where(lane == 1, hi[:, None], 0))
    send_ids = lax.all_to_all(request, "space", 0, 0, tiled=True)[:, :2]
    slot = jnp.where(local_id == lo[run_of], 0, 1)

    pick = jnp.where(remote, run_of * 2 + slot, 0)

    def exchange(sent):
        return lax.all_to_all(sent, "space", 0, 0, tiled=True)

    tiles = tiles.transpose(0, 1, 3, 2).reshape(tile_rows, kept * TILE, TILE)
    send_ids, tiles, pick = lax.optimization_barrier((send_ids, tiles, pick))
    total_sites = site_count * space_count
    first_site = me * site_count
    lookup = (neighbours - first_site + TILE) % total_sites
    parity_sign = jnp.where(lax.axis_index("tm") == 0, -1.0, 1.0).astype(jnp.float32)
    widened = with_halo(solution, (("space", 1),), TILE)
    blocks = site_count // TILE
    starts = (jnp.arange(blocks, dtype=jnp.int32) * TILE)[:, None, None]
    offsets = lookup.reshape(3, blocks, TILE).transpose(1, 0, 2) - starts
    window = jnp.arange(3 * TILE, dtype=jnp.int32)[None, None, :, None]
    adjacency = jnp.sum((offsets[:, :, None, :] == window).astype(jnp.float32), axis=1)
    parts = widened.reshape(slices, blocks + 2, TILE)
    windows = jnp.concatenate([parts[:, :-2], parts[:, 1:-1], parts[:, 2:]], axis=2)
    beside = jnp.einsum("tbj,bji->tbi", windows, adjacency, precision=lax.Precision.HIGHEST)
    hopped = solution + hop_kappa * beside.reshape(slices, site_count)
    own = field.reshape(slices, tile_rows, TILE)
    first = jnp.take(own, send_ids.reshape(-1), axis=1, mode="clip").transpose(1, 0, 2)
    got = exchange(first)
    moment, field_one, sent = substep(field, momentum, got, tiles, pick, send_ids, 0.5 * step_size, True, True)
    arrived = from_behind(hopped[-1:], "tm", 1)
    got = exchange(sent)
    moment, field_two, sent = substep(field_one, moment, got, tiles, pick, send_ids, step_size, True, True)
    sent, arrived = lax.optimization_barrier((sent, arrived))
    got = exchange(sent)
    (moment,) = substep(field_two, moment, got, tiles, pick, send_ids, 0.5 * step_size, False, False)

    earlier = jnp.concatenate([parity_sign * arrived, hopped[:-1]], axis=0)
    link_factor = jnp.exp(coupling * field_two)
    shifted = solution - link_factor * earlier
    force = 2.0 * coupling * shifted * link_factor * earlier
    return (field_two, moment, force)


def solution(mesh):
    in_specs = (
        P("tm", "space"),
        P("tm", "space"),
        P("tm", "space"),
        P("space", None, None, None),
        P("space", None),
        P(None, "space"),
    )
    out_specs = (P("tm", "space"), P("tm", "space"), P("tm", "space"))
    return jax.shard_map(body, mesh=mesh, in_specs=in_specs, out_specs=out_specs, check_vma=False)
```

```python
import jax
import jax.numpy as jnp
from jax import lax
from jax.sharding import PartitionSpec as P
from jax.experimental import pallas as pl
from jax.experimental.pallas import tpu as pltpu

TILE = 128


step_size = 0.5
hop_kappa = 0.5
coupling = 0.25


def with_halo(block, sides, width):
    for axis, dim in sides:
        count = lax.axis_size(axis)
        forward = [(i, i + 1) for i in range(count - 1)]
        forward.append((count - 1, 0))
        backward = [(target, source) for source, target in forward]
        low = lax.ppermute(
            lax.slice_in_dim(block, block.shape[dim] - width, None, axis=dim), axis, forward
        )
        high = lax.ppermute(lax.slice_in_dim(block, 0, width, axis=dim), axis, backward)
        block = jnp.concatenate([low, block, high], axis=dim)
    return block


def from_behind(value, axis, steps):
    count = lax.axis_size(axis)
    pairs = [(source, (source + steps) % count) for source in range(count)]
    return lax.ppermute(value, axis, pairs)


def split_dot(a, b):
    a_hi = a.astype(jnp.bfloat16)
    a_lo = (a - a_hi.astype(jnp.float32)).astype(jnp.bfloat16)
    b_hi = b.astype(jnp.bfloat16)
    b_lo = (b - b_hi.astype(jnp.float32)).astype(jnp.bfloat16)

    def part(x, y):
        return jnp.dot(x, y, preferred_element_type=jnp.float32)

    return part(a_hi, b_hi) + (part(a_hi, b_lo) + part(a_lo, b_hi))


def substep(field, moment, got, tiles, pick, send_ids, scale, advance, send, local=None):
    slices, site_count = field.shape
    rows = tiles.shape[0]
    kept = tiles.shape[1] // TILE + (0 if local is None else 1)
    slots = send_ids.shape[0] * send_ids.shape[1]

    def kernel(pick_ref, sid_ref, f_ref, p_ref, got_ref, tiles_ref, *refs):
        outs = list(refs)
        local_ref = outs.pop(0) if local is not None else None
        p_out = outs.pop(0)
        f_out = outs.pop(0) if advance else None
        send_out = outs.pop(0) if send else None
        held = outs.pop(0) if send else None
        for r in range(rows):
            cols = slice(r * TILE, (r + 1) * TILE)
            pieces = [got_ref[pick_ref[r, k]] for k in range(1, kept)]
            if local is None:
                acc = split_dot(jnp.concatenate([f_ref[:, cols]] + pieces, axis=1), tiles_ref[r])
            else:
                acc = local_ref[:, cols] + split_dot(jnp.concatenate(pieces, axis=1), tiles_ref[r])
            p_new = p_ref[:, cols] - scale * acc
            p_out[:, cols] = p_new
            if advance:
                f_new = f_ref[:, cols] + step_size * p_new
                f_out[:, cols] = f_new
                if send:
                    held[r] = f_new
        if send:
            pair = sid_ref.shape[1]
            for s in range(slots):
                send_out[s] = held[sid_ref[s // pair, s % pair]]

    vmem = pl.BlockSpec(memory_space=pltpu.VMEM)
    smem = pl.BlockSpec(memory_space=pltpu.SMEM)
    out_shape = [jax.ShapeDtypeStruct(field.shape, jnp.float32)]
    if advance:
        out_shape.append(jax.ShapeDtypeStruct(field.shape, jnp.float32))
    scratch = []
    if send:
        out_shape.append(jax.ShapeDtypeStruct((slots, slices, TILE), jnp.float32))
        scratch.append(pltpu.VMEM((rows, slices, TILE), jnp.float32))
    return pl.pallas_call(
        kernel,
        out_shape=tuple(out_shape),
        in_specs=[smem, smem, vmem, vmem, vmem, vmem] + ([] if local is None else [vmem]),
        out_specs=tuple([vmem] * len(out_shape)),
        scratch_shapes=scratch,
    )(pick, send_ids, field, moment, got, tiles, *([] if local is None else [local]))


def body(field, momentum, solution, tiles, columns, neighbours):
    slices = field.shape[0]
    tile_rows = tiles.shape[0]
    kept = tiles.shape[1]
    site_count = field.shape[1]
    space_count = lax.axis_size("space")
    me = lax.axis_index("space")

    run_of = lax.div(columns, tile_rows)
    local_id = lax.rem(columns, tile_rows)
    remote = run_of != me
    runs = lax.broadcasted_iota(jnp.int32, (space_count, tile_rows * kept), 0)
    flat_run = jnp.where(remote, run_of, -1).reshape(1, -1)
    flat_id = local_id.reshape(1, -1)
    hit = flat_run == runs
    lo = jnp.min(jnp.where(hit, flat_id, tile_rows), axis=1)
    hi = jnp.max(jnp.where(hit, flat_id, -1), axis=1)
    lo = jnp.clip(lo, 0, tile_rows - 1)
    hi = jnp.clip(hi, 0, tile_rows - 1)
    lane = lax.broadcasted_iota(jnp.int32, (space_count, TILE), 1)
    request = jnp.where(lane == 0, lo[:, None], jnp.where(lane == 1, hi[:, None], 0))
    send_ids = lax.all_to_all(request, "space", 0, 0, tiled=True)[:, :2]
    slot = jnp.where(local_id == lo[run_of], 0, 1)

    pick = jnp.where(remote, run_of * 2 + slot, 0)

    def exchange(sent):
        return lax.all_to_all(sent, "space", 0, 0, tiled=True)

    own_tiles = tiles[:, 0]
    remote_tiles = tiles[:, 1:].transpose(0, 1, 3, 2).reshape(tile_rows, (kept - 1) * TILE, TILE)
    tiles = tiles.transpose(0, 1, 3, 2).reshape(tile_rows, kept * TILE, TILE)
    total_sites = site_count * space_count
    first_site = me * site_count
    lookup = (neighbours - first_site + TILE) % total_sites
    parity_sign = jnp.where(lax.axis_index("tm") == 0, -1.0, 1.0).astype(jnp.float32)
    widened = with_halo(solution, (("space", 1),), TILE)
    blocks = site_count // TILE
    starts = (jnp.arange(blocks, dtype=jnp.int32) * TILE)[:, None, None]
    offsets = lookup.reshape(3, blocks, TILE).transpose(1, 0, 2) - starts
    window = jnp.arange(3 * TILE, dtype=jnp.int32)[None, None, :, None]
    adjacency = jnp.sum((offsets[:, :, None, :] == window).astype(jnp.float32), axis=1)
    parts = widened.reshape(slices, blocks + 2, TILE)
    windows = jnp.concatenate([parts[:, :-2], parts[:, 1:-1], parts[:, 2:]], axis=2)
    beside = jnp.einsum("tbj,bji->tbi", windows, adjacency, precision=lax.Precision.HIGHEST)
    hopped = solution + hop_kappa * beside.reshape(slices, site_count)
    own = field.reshape(slices, tile_rows, TILE)
    first = jnp.take(own, send_ids.reshape(-1), axis=1, mode="clip").transpose(1, 0, 2)
    got = exchange(first)
    moment, field_one, sent = substep(field, momentum, got, tiles, pick, send_ids, 0.5 * step_size, True, True)
    arrived = from_behind(hopped[-1:], "tm", 1)
    got = exchange(sent)
    moment, field_two, sent = substep(field_one, moment, got, tiles, pick, send_ids, step_size, True, True)
    sent, arrived = lax.optimization_barrier((sent, arrived))
    got = exchange(sent)
    local = jnp.einsum(
        "rij,trj->tri", own_tiles, field_two.reshape(slices, tile_rows, TILE), precision=lax.Precision.HIGHEST
    ).reshape(slices, site_count)
    (moment,) = substep(
        field_two, moment, got, remote_tiles, pick, send_ids, 0.5 * step_size, False, False, local
    )

    earlier = jnp.concatenate([parity_sign * arrived, hopped[:-1]], axis=0)
    link_factor = jnp.exp(coupling * field_two)
    shifted = solution - link_factor * earlier
    force = 2.0 * coupling * shifted * link_factor * earlier
    return (field_two, moment, force)


def solution(mesh):
    in_specs = (
        P("tm", "space"),
        P("tm", "space"),
        P("tm", "space"),
        P("space", None, None, None),
        P("space", None),
        P(None, "space"),
    )
    out_specs = (P("tm", "space"), P("tm", "space"), P("tm", "space"))
    return jax.shard_map(body, mesh=mesh, in_specs=in_specs, out_specs=out_specs, check_vma=False)
```

```python
import jax
import jax.numpy as jnp
from jax import lax
from jax.sharding import PartitionSpec as P
from jax.experimental import pallas as pl
from jax.experimental.pallas import tpu as pltpu

TILE = 128


step_size = 0.5
hop_kappa = 0.5
coupling = 0.25


def with_halo(block, sides, width):
    for axis, dim in sides:
        count = lax.axis_size(axis)
        forward = [(i, i + 1) for i in range(count - 1)]
        forward.append((count - 1, 0))
        backward = [(target, source) for source, target in forward]
        low = lax.ppermute(
            lax.slice_in_dim(block, block.shape[dim] - width, None, axis=dim), axis, forward
        )
        high = lax.ppermute(lax.slice_in_dim(block, 0, width, axis=dim), axis, backward)
        block = jnp.concatenate([low, block, high], axis=dim)
    return block


def from_behind(value, axis, steps):
    count = lax.axis_size(axis)
    pairs = [(source, (source + steps) % count) for source in range(count)]
    return lax.ppermute(value, axis, pairs)


def split_dot(a, b):
    a_hi = a.astype(jnp.bfloat16)
    a_lo = (a - a_hi.astype(jnp.float32)).astype(jnp.bfloat16)
    b_hi = b.astype(jnp.bfloat16)
    b_lo = (b - b_hi.astype(jnp.float32)).astype(jnp.bfloat16)

    def part(x, y):
        return jnp.dot(x, y, preferred_element_type=jnp.float32)

    return part(a_hi, b_hi) + (part(a_hi, b_lo) + part(a_lo, b_hi))


def substep(field, moment, got, tiles, pick, send_ids, scale, advance, send, local=None):
    slices, site_count = field.shape
    rows = tiles.shape[0]
    kept = tiles.shape[1] // TILE + (0 if local is None else 1)
    slots = send_ids.shape[0] * send_ids.shape[1]

    def kernel(pick_ref, sid_ref, f_ref, p_ref, got_ref, tiles_ref, *refs):
        outs = list(refs)
        local_ref = outs.pop(0) if local is not None else None
        p_out = outs.pop(0)
        f_out = outs.pop(0) if advance else None
        send_out = outs.pop(0) if send else None
        held = outs.pop(0) if send else None
        for r in range(rows):
            cols = slice(r * TILE, (r + 1) * TILE)
            pieces = [got_ref[pick_ref[r, k]] for k in range(1, kept)]
            if local is None:
                acc = split_dot(jnp.concatenate([f_ref[:, cols]] + pieces, axis=1), tiles_ref[r])
            else:
                acc = local_ref[:, cols] + split_dot(jnp.concatenate(pieces, axis=1), tiles_ref[r])
            p_new = p_ref[:, cols] - scale * acc
            p_out[:, cols] = p_new
            if advance:
                f_new = f_ref[:, cols] + step_size * p_new
                f_out[:, cols] = f_new
                if send:
                    held[r] = f_new
        if send:
            pair = sid_ref.shape[1]
            for s in range(slots):
                send_out[s] = held[sid_ref[s // pair, s % pair]]

    vmem = pl.BlockSpec(memory_space=pltpu.VMEM)
    smem = pl.BlockSpec(memory_space=pltpu.SMEM)
    out_shape = [jax.ShapeDtypeStruct(field.shape, jnp.float32)]
    if advance:
        out_shape.append(jax.ShapeDtypeStruct(field.shape, jnp.float32))
    scratch = []
    if send:
        out_shape.append(jax.ShapeDtypeStruct((slots, slices, TILE), jnp.float32))
        scratch.append(pltpu.VMEM((rows, slices, TILE), jnp.float32))
    return pl.pallas_call(
        kernel,
        out_shape=tuple(out_shape),
        in_specs=[smem, smem, vmem, vmem, vmem, vmem] + ([] if local is None else [vmem]),
        out_specs=tuple([vmem] * len(out_shape)),
        scratch_shapes=scratch,
    )(pick, send_ids, field, moment, got, tiles, *([] if local is None else [local]))


def body(field, momentum, solution, tiles, columns, neighbours):
    slices = field.shape[0]
    tile_rows = tiles.shape[0]
    kept = tiles.shape[1]
    site_count = field.shape[1]
    space_count = lax.axis_size("space")
    me = lax.axis_index("space")

    run_of = lax.div(columns, tile_rows)
    local_id = lax.rem(columns, tile_rows)
    remote = run_of != me
    runs = lax.broadcasted_iota(jnp.int32, (space_count, tile_rows * kept), 0)
    flat_run = jnp.where(remote, run_of, -1).reshape(1, -1)
    flat_id = local_id.reshape(1, -1)
    hit = flat_run == runs
    lo = jnp.min(jnp.where(hit, flat_id, tile_rows), axis=1)
    hi = jnp.max(jnp.where(hit, flat_id, -1), axis=1)
    lo = jnp.clip(lo, 0, tile_rows - 1)
    hi = jnp.clip(hi, 0, tile_rows - 1)
    lane = lax.broadcasted_iota(jnp.int32, (space_count, TILE), 1)
    request = jnp.where(lane == 0, lo[:, None], jnp.where(lane == 1, hi[:, None], 0))
    send_ids = lax.all_to_all(request, "space", 0, 0, tiled=True)[:, :2]
    slot = jnp.where(local_id == lo[run_of], 0, 1)

    pick = jnp.where(remote, run_of * 2 + slot, 0)

    def exchange(sent):
        return lax.all_to_all(sent, "space", 0, 0, tiled=True)

    own_tiles = tiles[:, 0]
    remote_tiles = tiles[:, 1:].transpose(0, 1, 3, 2).reshape(tile_rows, (kept - 1) * TILE, TILE)
    tiles = tiles.transpose(0, 1, 3, 2).reshape(tile_rows, kept * TILE, TILE)
    total_sites = site_count * space_count
    first_site = me * site_count
    lookup = (neighbours - first_site + TILE) % total_sites
    parity_sign = jnp.where(lax.axis_index("tm") == 0, -1.0, 1.0).astype(jnp.float32)
    widened = with_halo(solution, (("space", 1),), TILE)
    blocks = site_count // TILE
    starts = (jnp.arange(blocks, dtype=jnp.int32) * TILE)[:, None, None]
    offsets = lookup.reshape(3, blocks, TILE).transpose(1, 0, 2) - starts
    window = jnp.arange(3 * TILE, dtype=jnp.int32)[None, None, :, None]
    adjacency = jnp.sum((offsets[:, :, None, :] == window).astype(jnp.float32), axis=1)
    parts = widened.reshape(slices, blocks + 2, TILE)
    windows = jnp.concatenate([parts[:, :-2], parts[:, 1:-1], parts[:, 2:]], axis=2)
    beside = jnp.einsum("tbj,bji->tbi", windows, adjacency, precision=lax.Precision.HIGHEST)
    hopped = solution + hop_kappa * beside.reshape(slices, site_count)
    own = field.reshape(slices, tile_rows, TILE)
    first = jnp.take(own, send_ids.reshape(-1), axis=1, mode="clip").transpose(1, 0, 2)
    got = exchange(first)
    moment, field_one, sent = substep(field, momentum, got, tiles, pick, send_ids, 0.5 * step_size, True, True)
    arrived = from_behind(hopped[-1:], "tm", 1)
    got = exchange(sent)
    local = jnp.einsum(
        "rij,trj->tri", own_tiles, field_one.reshape(slices, tile_rows, TILE), precision=lax.Precision.HIGHEST
    ).reshape(slices, site_count)
    moment, field_two, sent = substep(
        field_one, moment, got, remote_tiles, pick, send_ids, step_size, True, True, local
    )
    sent, arrived = lax.optimization_barrier((sent, arrived))
    got = exchange(sent)
    local = jnp.einsum(
        "rij,trj->tri", own_tiles, field_two.reshape(slices, tile_rows, TILE), precision=lax.Precision.HIGHEST
    ).reshape(slices, site_count)
    (moment,) = substep(
        field_two, moment, got, remote_tiles, pick, send_ids, 0.5 * step_size, False, False, local
    )

    earlier = jnp.concatenate([parity_sign * arrived, hopped[:-1]], axis=0)
    link_factor = jnp.exp(coupling * field_two)
    shifted = solution - link_factor * earlier
    force = 2.0 * coupling * shifted * link_factor * earlier
    return (field_two, moment, force)


def solution(mesh):
    in_specs = (
        P("tm", "space"),
        P("tm", "space"),
        P("tm", "space"),
        P("space", None, None, None),
        P("space", None),
        P(None, "space"),
    )
    out_specs = (P("tm", "space"), P("tm", "space"), P("tm", "space"))
    return jax.shard_map(body, mesh=mesh, in_specs=in_specs, out_specs=out_specs, check_vma=False)
```

```python
import jax
import jax.numpy as jnp
from jax import lax
from jax.sharding import PartitionSpec as P
from jax.experimental import pallas as pl
from jax.experimental.pallas import tpu as pltpu

TILE = 128


step_size = 0.5
hop_kappa = 0.5
coupling = 0.25


def with_halo(block, sides, width):
    for axis, dim in sides:
        count = lax.axis_size(axis)
        forward = [(i, i + 1) for i in range(count - 1)]
        forward.append((count - 1, 0))
        backward = [(target, source) for source, target in forward]
        low = lax.ppermute(
            lax.slice_in_dim(block, block.shape[dim] - width, None, axis=dim), axis, forward
        )
        high = lax.ppermute(lax.slice_in_dim(block, 0, width, axis=dim), axis, backward)
        block = jnp.concatenate([low, block, high], axis=dim)
    return block


def from_behind(value, axis, steps):
    count = lax.axis_size(axis)
    pairs = [(source, (source + steps) % count) for source in range(count)]
    return lax.ppermute(value, axis, pairs)


def split_dot(a, b):
    a_hi = a.astype(jnp.bfloat16)
    a_lo = (a - a_hi.astype(jnp.float32)).astype(jnp.bfloat16)
    b_hi = b.astype(jnp.bfloat16)
    b_lo = (b - b_hi.astype(jnp.float32)).astype(jnp.bfloat16)

    def part(x, y):
        return jnp.dot(x, y, preferred_element_type=jnp.float32)

    return part(a_hi, b_hi) + (part(a_hi, b_lo) + part(a_lo, b_hi))


def substep(field, moment, got, tiles, pick, send_ids, scale, advance, send, local=None):
    slices, site_count = field.shape
    rows, kept = tiles.shape[0], pick.shape[1]
    offset = tiles.shape[1] - (kept - 1) * TILE
    slots = send_ids.shape[0] * send_ids.shape[1]

    def kernel(pick_ref, sid_ref, f_ref, p_ref, got_ref, tiles_ref, *refs):
        outs = list(refs)
        local_ref = outs.pop(0) if local is not None else None
        p_out = outs.pop(0)
        f_out = outs.pop(0) if advance else None
        send_out = outs.pop(0) if send else None
        held = outs.pop(0) if send else None
        for r in range(rows):
            cols = slice(r * TILE, (r + 1) * TILE)
            pieces = [got_ref[pick_ref[r, k]] for k in range(1, kept)]
            if local is None:
                acc = split_dot(jnp.concatenate([f_ref[:, cols]] + pieces, axis=1), tiles_ref[r])
            else:
                acc = local_ref[:, cols] + split_dot(jnp.concatenate(pieces, axis=1), tiles_ref[r, offset:, :])
            p_new = p_ref[:, cols] - scale * acc
            p_out[:, cols] = p_new
            if advance:
                f_new = f_ref[:, cols] + step_size * p_new
                f_out[:, cols] = f_new
                if send:
                    held[r] = f_new
        if send:
            pair = sid_ref.shape[1]
            for s in range(slots):
                send_out[s] = held[sid_ref[s // pair, s % pair]]

    vmem = pl.BlockSpec(memory_space=pltpu.VMEM)
    smem = pl.BlockSpec(memory_space=pltpu.SMEM)
    out_shape = [jax.ShapeDtypeStruct(field.shape, jnp.float32)]
    if advance:
        out_shape.append(jax.ShapeDtypeStruct(field.shape, jnp.float32))
    scratch = []
    if send:
        out_shape.append(jax.ShapeDtypeStruct((slots, slices, TILE), jnp.float32))
        scratch.append(pltpu.VMEM((rows, slices, TILE), jnp.float32))
    return pl.pallas_call(
        kernel,
        out_shape=tuple(out_shape),
        in_specs=[smem, smem, vmem, vmem, vmem, vmem] + ([] if local is None else [vmem]),
        out_specs=tuple([vmem] * len(out_shape)),
        scratch_shapes=scratch,
    )(pick, send_ids, field, moment, got, tiles, *([] if local is None else [local]))


def body(field, momentum, solution, tiles, columns, neighbours):
    slices = field.shape[0]
    tile_rows = tiles.shape[0]
    kept = tiles.shape[1]
    site_count = field.shape[1]
    space_count = lax.axis_size("space")
    me = lax.axis_index("space")

    run_of = lax.div(columns, tile_rows)
    local_id = lax.rem(columns, tile_rows)
    remote = run_of != me
    runs = lax.broadcasted_iota(jnp.int32, (space_count, tile_rows * kept), 0)
    flat_run = jnp.where(remote, run_of, -1).reshape(1, -1)
    flat_id = local_id.reshape(1, -1)
    hit = flat_run == runs
    lo = jnp.min(jnp.where(hit, flat_id, tile_rows), axis=1)
    hi = jnp.max(jnp.where(hit, flat_id, -1), axis=1)
    lo = jnp.clip(lo, 0, tile_rows - 1)
    hi = jnp.clip(hi, 0, tile_rows - 1)
    lane = lax.broadcasted_iota(jnp.int32, (space_count, TILE), 1)
    request = jnp.where(lane == 0, lo[:, None], jnp.where(lane == 1, hi[:, None], 0))
    send_ids = lax.all_to_all(request, "space", 0, 0, tiled=True)[:, :2]
    slot = jnp.where(local_id == lo[run_of], 0, 1)

    pick = jnp.where(remote, run_of * 2 + slot, 0)

    def exchange(sent):
        return lax.all_to_all(sent, "space", 0, 0, tiled=True)

    own_tiles = tiles[:, 0]
    remote_tiles = tiles[:, 1:].transpose(0, 1, 3, 2).reshape(tile_rows, (kept - 1) * TILE, TILE)
    tiles = tiles.transpose(0, 1, 3, 2).reshape(tile_rows, kept * TILE, TILE)
    total_sites = site_count * space_count
    first_site = me * site_count
    lookup = (neighbours - first_site + TILE) % total_sites
    parity_sign = jnp.where(lax.axis_index("tm") == 0, -1.0, 1.0).astype(jnp.float32)
    widened = with_halo(solution, (("space", 1),), TILE)
    blocks = site_count // TILE
    starts = (jnp.arange(blocks, dtype=jnp.int32) * TILE)[:, None, None]
    offsets = lookup.reshape(3, blocks, TILE).transpose(1, 0, 2) - starts
    window = jnp.arange(3 * TILE, dtype=jnp.int32)[None, None, :, None]
    adjacency = jnp.sum((offsets[:, :, None, :] == window).astype(jnp.float32), axis=1)
    parts = widened.reshape(slices, blocks + 2, TILE)
    windows = jnp.concatenate([parts[:, :-2], parts[:, 1:-1], parts[:, 2:]], axis=2)
    beside = jnp.einsum("tbj,bji->tbi", windows, adjacency, precision=lax.Precision.HIGHEST)
    hopped = solution + hop_kappa * beside.reshape(slices, site_count)
    own = field.reshape(slices, tile_rows, TILE)
    first = jnp.take(own, send_ids.reshape(-1), axis=1, mode="clip").transpose(1, 0, 2)
    got = exchange(first)
    moment, field_one, sent = substep(field, momentum, got, tiles, pick, send_ids, 0.5 * step_size, True, True)
    arrived = from_behind(hopped[-1:], "tm", 1)
    got = exchange(sent)
    local = jnp.einsum(
        "rij,trj->tri", own_tiles, field_one.reshape(slices, tile_rows, TILE), precision=lax.Precision.HIGHEST
    ).reshape(slices, site_count)
    moment, field_two, sent = substep(
        field_one, moment, got, tiles, pick, send_ids, step_size, True, True, local
    )
    sent, arrived = lax.optimization_barrier((sent, arrived))
    got = exchange(sent)
    local = jnp.einsum(
        "rij,trj->tri", own_tiles, field_two.reshape(slices, tile_rows, TILE), precision=lax.Precision.HIGHEST
    ).reshape(slices, site_count)
    (moment,) = substep(
        field_two, moment, got, remote_tiles, pick, send_ids, 0.5 * step_size, False, False, local
    )

    earlier = jnp.concatenate([parity_sign * arrived, hopped[:-1]], axis=0)
    link_factor = jnp.exp(coupling * field_two)
    shifted = solution - link_factor * earlier
    force = 2.0 * coupling * shifted * link_factor * earlier
    return (field_two, moment, force)


def solution(mesh):
    in_specs = (
        P("tm", "space"),
        P("tm", "space"),
        P("tm", "space"),
        P("space", None, None, None),
        P("space", None),
        P(None, "space"),
    )
    out_specs = (P("tm", "space"), P("tm", "space"), P("tm", "space"))
    return jax.shard_map(body, mesh=mesh, in_specs=in_specs, out_specs=out_specs, check_vma=False)
```

```python
import jax
import jax.numpy as jnp
from jax import lax
from jax.sharding import PartitionSpec as P
from jax.experimental import pallas as pl
from jax.experimental.pallas import tpu as pltpu

TILE = 128


step_size = 0.5
hop_kappa = 0.5
coupling = 0.25


def with_halo(block, sides, width):
    for axis, dim in sides:
        count = lax.axis_size(axis)
        forward = [(i, i + 1) for i in range(count - 1)]
        forward.append((count - 1, 0))
        backward = [(target, source) for source, target in forward]
        low = lax.ppermute(
            lax.slice_in_dim(block, block.shape[dim] - width, None, axis=dim), axis, forward
        )
        high = lax.ppermute(lax.slice_in_dim(block, 0, width, axis=dim), axis, backward)
        block = jnp.concatenate([low, block, high], axis=dim)
    return block


def from_behind(value, axis, steps):
    count = lax.axis_size(axis)
    pairs = [(source, (source + steps) % count) for source in range(count)]
    return lax.ppermute(value, axis, pairs)


def split_dot(a, b):
    a_hi = a.astype(jnp.bfloat16)
    a_lo = (a - a_hi.astype(jnp.float32)).astype(jnp.bfloat16)
    b_hi = b.astype(jnp.bfloat16)
    b_lo = (b - b_hi.astype(jnp.float32)).astype(jnp.bfloat16)

    def part(x, y):
        return jnp.dot(x, y, preferred_element_type=jnp.float32)

    return part(a_hi, b_hi) + (part(a_hi, b_lo) + part(a_lo, b_hi))


def substep(field, moment, got, tiles, pick, send_ids, scale, advance, send, local=None):
    slices, site_count = field.shape
    rows, kept = tiles.shape[0], pick.shape[1]
    offset = tiles.shape[1] - (kept - 1) * TILE
    slots = send_ids.shape[0] * send_ids.shape[1]

    def kernel(pick_ref, sid_ref, f_ref, p_ref, got_ref, tiles_ref, *refs):
        outs = list(refs)
        local_ref = outs.pop(0) if local is not None else None
        p_out = outs.pop(0)
        f_out = outs.pop(0) if advance else None
        send_out = outs.pop(0) if send else None
        held = outs.pop(0) if send else None
        for r in range(rows):
            cols = slice(r * TILE, (r + 1) * TILE)
            pieces = [got_ref[pick_ref[r, k]] for k in range(1, kept)]
            if local is None:
                acc = split_dot(jnp.concatenate([f_ref[:, cols]] + pieces, axis=1), tiles_ref[r])
            else:
                acc = local_ref[:, cols] + split_dot(jnp.concatenate(pieces, axis=1), tiles_ref[r, offset:, :])
            p_new = p_ref[:, cols] - scale * acc
            p_out[:, cols] = p_new
            if advance:
                f_new = f_ref[:, cols] + step_size * p_new
                f_out[:, cols] = f_new
                if send:
                    held[r] = f_new
        if send:
            pair = sid_ref.shape[1]
            for s in range(slots):
                send_out[s] = held[sid_ref[s // pair, s % pair]]

    vmem = pl.BlockSpec(memory_space=pltpu.VMEM)
    smem = pl.BlockSpec(memory_space=pltpu.SMEM)
    out_shape = [jax.ShapeDtypeStruct(field.shape, jnp.float32)]
    if advance:
        out_shape.append(jax.ShapeDtypeStruct(field.shape, jnp.float32))
    scratch = []
    if send:
        out_shape.append(jax.ShapeDtypeStruct((slots, slices, TILE), jnp.float32))
        scratch.append(pltpu.VMEM((rows, slices, TILE), jnp.float32))
    return pl.pallas_call(
        kernel,
        out_shape=tuple(out_shape),
        in_specs=[smem, smem, vmem, vmem, vmem, vmem] + ([] if local is None else [vmem]),
        out_specs=tuple([vmem] * len(out_shape)),
        scratch_shapes=scratch,
    )(pick, send_ids, field, moment, got, tiles, *([] if local is None else [local]))


def body(field, momentum, solution, tiles, columns, neighbours):
    slices = field.shape[0]
    tile_rows = tiles.shape[0]
    kept = tiles.shape[1]
    site_count = field.shape[1]
    space_count = lax.axis_size("space")
    me = lax.axis_index("space")

    run_of = lax.div(columns, tile_rows)
    local_id = lax.rem(columns, tile_rows)
    remote = run_of != me
    runs = lax.broadcasted_iota(jnp.int32, (space_count, tile_rows * kept), 0)
    flat_run = jnp.where(remote, run_of, -1).reshape(1, -1)
    flat_id = local_id.reshape(1, -1)
    hit = flat_run == runs
    lo = jnp.min(jnp.where(hit, flat_id, tile_rows), axis=1)
    hi = jnp.max(jnp.where(hit, flat_id, -1), axis=1)
    lo = jnp.clip(lo, 0, tile_rows - 1)
    hi = jnp.clip(hi, 0, tile_rows - 1)
    lane = lax.broadcasted_iota(jnp.int32, (space_count, TILE), 1)
    request = jnp.where(lane == 0, lo[:, None], jnp.where(lane == 1, hi[:, None], 0))
    send_ids = lax.all_to_all(request, "space", 0, 0, tiled=True)[:, :2]
    slot = jnp.where(local_id == lo[run_of], 0, 1)

    pick = jnp.where(remote, run_of * 2 + slot, 0)

    def exchange(sent):
        return lax.all_to_all(sent, "space", 0, 0, tiled=True)

    own_tiles = tiles[:, 0]
    remote_tiles = tiles[:, 1:].transpose(0, 1, 3, 2).reshape(tile_rows, (kept - 1) * TILE, TILE)
    tiles = tiles.transpose(0, 1, 3, 2).reshape(tile_rows, kept * TILE, TILE)
    total_sites = site_count * space_count
    first_site = me * site_count
    lookup = (neighbours - first_site + TILE) % total_sites
    parity_sign = jnp.where(lax.axis_index("tm") == 0, -1.0, 1.0).astype(jnp.float32)
    widened = with_halo(solution, (("space", 1),), TILE)
    blocks = site_count // TILE
    starts = (jnp.arange(blocks, dtype=jnp.int32) * TILE)[:, None, None]
    offsets = lookup.reshape(3, blocks, TILE).transpose(1, 0, 2) - starts
    window = jnp.arange(3 * TILE, dtype=jnp.int32)[None, None, :, None]
    adjacency = jnp.sum((offsets[:, :, None, :] == window).astype(jnp.float32), axis=1)
    parts = widened.reshape(slices, blocks + 2, TILE)
    windows = jnp.concatenate([parts[:, :-2], parts[:, 1:-1], parts[:, 2:]], axis=2)
    beside = jnp.einsum("tbj,bji->tbi", windows, adjacency, precision=lax.Precision.HIGHEST)
    hopped = solution + hop_kappa * beside.reshape(slices, site_count)
    own = field.reshape(slices, tile_rows, TILE)
    first = jnp.take(own, send_ids.reshape(-1), axis=1, mode="clip").transpose(1, 0, 2)
    got = exchange(first)
    held_field, _ = lax.optimization_barrier((field, send_ids))
    local = jnp.einsum(
        "rij,trj->tri", own_tiles, held_field.reshape(slices, tile_rows, TILE), precision=lax.Precision.HIGHEST
    ).reshape(slices, site_count)
    moment, field_one, sent = substep(
        field, momentum, got, tiles, pick, send_ids, 0.5 * step_size, True, True, local
    )
    arrived = from_behind(hopped[-1:], "tm", 1)
    got = exchange(sent)
    local = jnp.einsum(
        "rij,trj->tri", own_tiles, field_one.reshape(slices, tile_rows, TILE), precision=lax.Precision.HIGHEST
    ).reshape(slices, site_count)
    moment, field_two, sent = substep(
        field_one, moment, got, tiles, pick, send_ids, step_size, True, True, local
    )
    sent, arrived = lax.optimization_barrier((sent, arrived))
    got = exchange(sent)
    local = jnp.einsum(
        "rij,trj->tri", own_tiles, field_two.reshape(slices, tile_rows, TILE), precision=lax.Precision.HIGHEST
    ).reshape(slices, site_count)
    (moment,) = substep(
        field_two, moment, got, remote_tiles, pick, send_ids, 0.5 * step_size, False, False, local
    )

    earlier = jnp.concatenate([parity_sign * arrived, hopped[:-1]], axis=0)
    link_factor = jnp.exp(coupling * field_two)
    shifted = solution - link_factor * earlier
    force = 2.0 * coupling * shifted * link_factor * earlier
    return (field_two, moment, force)


def solution(mesh):
    in_specs = (
        P("tm", "space"),
        P("tm", "space"),
        P("tm", "space"),
        P("space", None, None, None),
        P("space", None),
        P(None, "space"),
    )
    out_specs = (P("tm", "space"), P("tm", "space"), P("tm", "space"))
    return jax.shard_map(body, mesh=mesh, in_specs=in_specs, out_specs=out_specs, check_vma=False)
```

```python
import jax
import jax.numpy as jnp
from jax import lax
from jax.sharding import PartitionSpec as P
from jax.experimental import pallas as pl
from jax.experimental.pallas import tpu as pltpu

TILE = 128


step_size = 0.5
hop_kappa = 0.5
coupling = 0.25


def with_halo(block, sides, width):
    for axis, dim in sides:
        count = lax.axis_size(axis)
        forward = [(i, i + 1) for i in range(count - 1)]
        forward.append((count - 1, 0))
        backward = [(target, source) for source, target in forward]
        low = lax.ppermute(
            lax.slice_in_dim(block, block.shape[dim] - width, None, axis=dim), axis, forward
        )
        high = lax.ppermute(lax.slice_in_dim(block, 0, width, axis=dim), axis, backward)
        block = jnp.concatenate([low, block, high], axis=dim)
    return block


def from_behind(value, axis, steps):
    count = lax.axis_size(axis)
    pairs = [(source, (source + steps) % count) for source in range(count)]
    return lax.ppermute(value, axis, pairs)


def split_dot(a, b):
    a_hi = a.astype(jnp.bfloat16)
    a_lo = (a - a_hi.astype(jnp.float32)).astype(jnp.bfloat16)
    b_hi = b.astype(jnp.bfloat16)
    b_lo = (b - b_hi.astype(jnp.float32)).astype(jnp.bfloat16)

    def part(x, y):
        return jnp.dot(x, y, preferred_element_type=jnp.float32)

    return part(a_hi, b_hi) + (part(a_hi, b_lo) + part(a_lo, b_hi))


def substep(field, moment, got, tiles, pick, send_ids, scale, advance, send, local=None):
    slices, site_count = field.shape
    rows = tiles.shape[0]
    kept = tiles.shape[1] // TILE + (0 if local is None else 1)
    slots = send_ids.shape[0] * send_ids.shape[1]

    def kernel(pick_ref, sid_ref, f_ref, p_ref, got_ref, tiles_ref, *refs):
        outs = list(refs)
        local_ref = outs.pop(0) if local is not None else None
        p_out = outs.pop(0)
        f_out = outs.pop(0) if advance else None
        send_out = outs.pop(0) if send else None
        held = outs.pop(0) if send else None
        for r in range(rows):
            cols = slice(r * TILE, (r + 1) * TILE)
            pieces = [got_ref[pick_ref[r, k]] for k in range(1, kept)]
            if local is None:
                acc = split_dot(jnp.concatenate([f_ref[:, cols]] + pieces, axis=1), tiles_ref[r])
            else:
                acc = local_ref[:, cols] + split_dot(jnp.concatenate(pieces, axis=1), tiles_ref[r])
            p_new = p_ref[:, cols] - scale * acc
            p_out[:, cols] = p_new
            if advance:
                f_new = f_ref[:, cols] + step_size * p_new
                f_out[:, cols] = f_new
                if send:
                    held[r] = f_new
        if send:
            pair = sid_ref.shape[1]
            for s in range(slots):
                send_out[s] = held[sid_ref[s // pair, s % pair]]

    vmem = pl.BlockSpec(memory_space=pltpu.VMEM)
    smem = pl.BlockSpec(memory_space=pltpu.SMEM)
    out_shape = [jax.ShapeDtypeStruct(field.shape, jnp.float32)]
    if advance:
        out_shape.append(jax.ShapeDtypeStruct(field.shape, jnp.float32))
    scratch = []
    if send:
        out_shape.append(jax.ShapeDtypeStruct((slots, slices, TILE), jnp.float32))
        scratch.append(pltpu.VMEM((rows, slices, TILE), jnp.float32))
    return pl.pallas_call(
        kernel,
        out_shape=tuple(out_shape),
        in_specs=[smem, smem, vmem, vmem, vmem, vmem] + ([] if local is None else [vmem]),
        out_specs=tuple([vmem] * len(out_shape)),
        scratch_shapes=scratch,
    )(pick, send_ids, field, moment, got, tiles, *([] if local is None else [local]))


def body(field, momentum, solution, tiles, columns, neighbours):
    slices = field.shape[0]
    tile_rows = tiles.shape[0]
    kept = tiles.shape[1]
    site_count = field.shape[1]
    space_count = lax.axis_size("space")
    me = lax.axis_index("space")

    run_of = lax.div(columns, tile_rows)
    local_id = lax.rem(columns, tile_rows)
    remote = run_of != me
    runs = lax.broadcasted_iota(jnp.int32, (space_count, tile_rows * kept), 0)
    flat_run = jnp.where(remote, run_of, -1).reshape(1, -1)
    flat_id = local_id.reshape(1, -1)
    hit = flat_run == runs
    lo = jnp.min(jnp.where(hit, flat_id, tile_rows), axis=1)
    hi = jnp.max(jnp.where(hit, flat_id, -1), axis=1)
    lo = jnp.clip(lo, 0, tile_rows - 1)
    hi = jnp.clip(hi, 0, tile_rows - 1)
    lane = lax.broadcasted_iota(jnp.int32, (space_count, TILE), 1)
    request = jnp.where(lane == 0, lo[:, None], jnp.where(lane == 1, hi[:, None], 0))
    send_ids = lax.all_to_all(request, "space", 0, 0, tiled=True)[:, :2]
    slot = jnp.where(local_id == lo[run_of], 0, 1)

    pick = jnp.where(remote, run_of * 2 + slot, 0)

    def exchange(sent):
        return lax.all_to_all(sent, "space", 0, 0, tiled=True)

    own_tiles = tiles[:, 0]
    remote_tiles = tiles[:, 1:].transpose(0, 1, 3, 2).reshape(tile_rows, (kept - 1) * TILE, TILE)
    tiles = tiles.transpose(0, 1, 3, 2).reshape(tile_rows, kept * TILE, TILE)
    total_sites = site_count * space_count
    first_site = me * site_count
    lookup = (neighbours - first_site + TILE) % total_sites
    parity_sign = jnp.where(lax.axis_index("tm") == 0, -1.0, 1.0).astype(jnp.float32)
    own = field.reshape(slices, tile_rows, TILE)
    first = jnp.take(own, send_ids.reshape(-1), axis=1, mode="clip").transpose(1, 0, 2)
    got = exchange(first)
    moment, field_one, sent = substep(field, momentum, got, tiles, pick, send_ids, 0.5 * step_size, True, True)
    sent, held_solution = lax.optimization_barrier((sent, solution))
    widened = with_halo(held_solution, (("space", 1),), TILE)
    blocks = site_count // TILE
    starts = (jnp.arange(blocks, dtype=jnp.int32) * TILE)[:, None, None]
    offsets = lookup.reshape(3, blocks, TILE).transpose(1, 0, 2) - starts
    window = jnp.arange(3 * TILE, dtype=jnp.int32)[None, None, :, None]
    adjacency = jnp.sum((offsets[:, :, None, :] == window).astype(jnp.float32), axis=1)
    parts = widened.reshape(slices, blocks + 2, TILE)
    windows = jnp.concatenate([parts[:, :-2], parts[:, 1:-1], parts[:, 2:]], axis=2)
    beside = jnp.einsum("tbj,bji->tbi", windows, adjacency, precision=lax.Precision.HIGHEST)
    hopped = solution + hop_kappa * beside.reshape(slices, site_count)
    arrived = from_behind(hopped[-1:], "tm", 1)
    got = exchange(sent)
    moment, field_two, sent = substep(field_one, moment, got, tiles, pick, send_ids, step_size, True, True)
    sent, arrived = lax.optimization_barrier((sent, arrived))
    got = exchange(sent)
    local = jnp.einsum(
        "rij,trj->tri", own_tiles, field_two.reshape(slices, tile_rows, TILE), precision=lax.Precision.HIGHEST
    ).reshape(slices, site_count)
    (moment,) = substep(
        field_two, moment, got, remote_tiles, pick, send_ids, 0.5 * step_size, False, False, local
    )

    earlier = jnp.concatenate([parity_sign * arrived, hopped[:-1]], axis=0)
    link_factor = jnp.exp(coupling * field_two)
    shifted = solution - link_factor * earlier
    force = 2.0 * coupling * shifted * link_factor * earlier
    return (field_two, moment, force)


def solution(mesh):
    in_specs = (
        P("tm", "space"),
        P("tm", "space"),
        P("tm", "space"),
        P("space", None, None, None),
        P("space", None),
        P(None, "space"),
    )
    out_specs = (P("tm", "space"), P("tm", "space"), P("tm", "space"))
    return jax.shard_map(body, mesh=mesh, in_specs=in_specs, out_specs=out_specs, check_vma=False)
```

```python
import jax
import jax.numpy as jnp
from jax import lax
from jax.sharding import PartitionSpec as P
from jax.experimental import pallas as pl
from jax.experimental.pallas import tpu as pltpu

TILE = 128


step_size = 0.5
hop_kappa = 0.5
coupling = 0.25


def with_halo(block, sides, width):
    for axis, dim in sides:
        count = lax.axis_size(axis)
        forward = [(i, i + 1) for i in range(count - 1)]
        forward.append((count - 1, 0))
        backward = [(target, source) for source, target in forward]
        low = lax.ppermute(
            lax.slice_in_dim(block, block.shape[dim] - width, None, axis=dim), axis, forward
        )
        high = lax.ppermute(lax.slice_in_dim(block, 0, width, axis=dim), axis, backward)
        block = jnp.concatenate([low, block, high], axis=dim)
    return block


def from_behind(value, axis, steps):
    count = lax.axis_size(axis)
    pairs = [(source, (source + steps) % count) for source in range(count)]
    return lax.ppermute(value, axis, pairs)


def split_dot(a, b):
    a_hi = a.astype(jnp.bfloat16)
    a_lo = (a - a_hi.astype(jnp.float32)).astype(jnp.bfloat16)
    b_hi = b.astype(jnp.bfloat16)
    b_lo = (b - b_hi.astype(jnp.float32)).astype(jnp.bfloat16)

    left = jnp.concatenate([a_hi, a_hi, a_lo], axis=1)
    right = jnp.concatenate([b_hi, b_lo, b_hi], axis=0)
    return jnp.dot(left, right, preferred_element_type=jnp.float32)


def substep(field, moment, got, tiles, pick, send_ids, scale, advance, send, local=None):
    slices, site_count = field.shape
    rows = tiles.shape[0]
    kept = tiles.shape[1] // TILE + (0 if local is None else 1)
    slots = send_ids.shape[0] * send_ids.shape[1]

    def kernel(pick_ref, sid_ref, f_ref, p_ref, got_ref, tiles_ref, *refs):
        outs = list(refs)
        local_ref = outs.pop(0) if local is not None else None
        p_out = outs.pop(0)
        f_out = outs.pop(0) if advance else None
        send_out = outs.pop(0) if send else None
        held = outs.pop(0) if send else None
        for r in range(rows):
            cols = slice(r * TILE, (r + 1) * TILE)
            pieces = [got_ref[pick_ref[r, k]] for k in range(1, kept)]
            if local is None:
                acc = split_dot(jnp.concatenate([f_ref[:, cols]] + pieces, axis=1), tiles_ref[r])
            else:
                acc = local_ref[:, cols] + split_dot(jnp.concatenate(pieces, axis=1), tiles_ref[r])
            p_new = p_ref[:, cols] - scale * acc
            p_out[:, cols] = p_new
            if advance:
                f_new = f_ref[:, cols] + step_size * p_new
                f_out[:, cols] = f_new
                if send:
                    held[r] = f_new
        if send:
            pair = sid_ref.shape[1]
            for s in range(slots):
                send_out[s] = held[sid_ref[s // pair, s % pair]]

    vmem = pl.BlockSpec(memory_space=pltpu.VMEM)
    smem = pl.BlockSpec(memory_space=pltpu.SMEM)
    out_shape = [jax.ShapeDtypeStruct(field.shape, jnp.float32)]
    if advance:
        out_shape.append(jax.ShapeDtypeStruct(field.shape, jnp.float32))
    scratch = []
    if send:
        out_shape.append(jax.ShapeDtypeStruct((slots, slices, TILE), jnp.float32))
        scratch.append(pltpu.VMEM((rows, slices, TILE), jnp.float32))
    return pl.pallas_call(
        kernel,
        out_shape=tuple(out_shape),
        in_specs=[smem, smem, vmem, vmem, vmem, vmem] + ([] if local is None else [vmem]),
        out_specs=tuple([vmem] * len(out_shape)),
        scratch_shapes=scratch,
    )(pick, send_ids, field, moment, got, tiles, *([] if local is None else [local]))


def body(field, momentum, solution, tiles, columns, neighbours):
    slices = field.shape[0]
    tile_rows = tiles.shape[0]
    kept = tiles.shape[1]
    site_count = field.shape[1]
    space_count = lax.axis_size("space")
    me = lax.axis_index("space")

    run_of = lax.div(columns, tile_rows)
    local_id = lax.rem(columns, tile_rows)
    remote = run_of != me
    runs = lax.broadcasted_iota(jnp.int32, (space_count, tile_rows * kept), 0)
    flat_run = jnp.where(remote, run_of, -1).reshape(1, -1)
    flat_id = local_id.reshape(1, -1)
    hit = flat_run == runs
    lo = jnp.min(jnp.where(hit, flat_id, tile_rows), axis=1)
    hi = jnp.max(jnp.where(hit, flat_id, -1), axis=1)
    lo = jnp.clip(lo, 0, tile_rows - 1)
    hi = jnp.clip(hi, 0, tile_rows - 1)
    lane = lax.broadcasted_iota(jnp.int32, (space_count, TILE), 1)
    request = jnp.where(lane == 0, lo[:, None], jnp.where(lane == 1, hi[:, None], 0))
    send_ids = lax.all_to_all(request, "space", 0, 0, tiled=True)[:, :2]
    slot = jnp.where(local_id == lo[run_of], 0, 1)

    pick = jnp.where(remote, run_of * 2 + slot, 0)

    def exchange(sent):
        return lax.all_to_all(sent, "space", 0, 0, tiled=True)

    own_tiles = tiles[:, 0]
    remote_tiles = tiles[:, 1:].transpose(0, 1, 3, 2).reshape(tile_rows, (kept - 1) * TILE, TILE)
    tiles = tiles.transpose(0, 1, 3, 2).reshape(tile_rows, kept * TILE, TILE)
    total_sites = site_count * space_count
    first_site = me * site_count
    lookup = (neighbours - first_site + TILE) % total_sites
    parity_sign = jnp.where(lax.axis_index("tm") == 0, -1.0, 1.0).astype(jnp.float32)
    widened = with_halo(solution, (("space", 1),), TILE)
    blocks = site_count // TILE
    starts = (jnp.arange(blocks, dtype=jnp.int32) * TILE)[:, None, None]
    offsets = lookup.reshape(3, blocks, TILE).transpose(1, 0, 2) - starts
    window = jnp.arange(3 * TILE, dtype=jnp.int32)[None, None, :, None]
    adjacency = jnp.sum((offsets[:, :, None, :] == window).astype(jnp.float32), axis=1)
    parts = widened.reshape(slices, blocks + 2, TILE)
    windows = jnp.concatenate([parts[:, :-2], parts[:, 1:-1], parts[:, 2:]], axis=2)
    beside = jnp.einsum("tbj,bji->tbi", windows, adjacency, precision=lax.Precision.HIGHEST)
    hopped = solution + hop_kappa * beside.reshape(slices, site_count)
    own = field.reshape(slices, tile_rows, TILE)
    first = jnp.take(own, send_ids.reshape(-1), axis=1, mode="clip").transpose(1, 0, 2)
    got = exchange(first)
    moment, field_one, sent = substep(field, momentum, got, tiles, pick, send_ids, 0.5 * step_size, True, True)
    arrived = from_behind(hopped[-1:], "tm", 1)
    got = exchange(sent)
    moment, field_two, sent = substep(field_one, moment, got, tiles, pick, send_ids, step_size, True, True)
    sent, arrived = lax.optimization_barrier((sent, arrived))
    got = exchange(sent)
    local = jnp.einsum(
        "rij,trj->tri", own_tiles, field_two.reshape(slices, tile_rows, TILE), precision=lax.Precision.HIGHEST
    ).reshape(slices, site_count)
    (moment,) = substep(
        field_two, moment, got, remote_tiles, pick, send_ids, 0.5 * step_size, False, False, local
    )

    earlier = jnp.concatenate([parity_sign * arrived, hopped[:-1]], axis=0)
    link_factor = jnp.exp(coupling * field_two)
    shifted = solution - link_factor * earlier
    force = 2.0 * coupling * shifted * link_factor * earlier
    return (field_two, moment, force)


def solution(mesh):
    in_specs = (
        P("tm", "space"),
        P("tm", "space"),
        P("tm", "space"),
        P("space", None, None, None),
        P("space", None),
        P(None, "space"),
    )
    out_specs = (P("tm", "space"), P("tm", "space"), P("tm", "space"))
    return jax.shard_map(body, mesh=mesh, in_specs=in_specs, out_specs=out_specs, check_vma=False)
```
